256 devices in a mesh: dp: 32 (over x, z), mp: 8 (over y, core).
Axes of the slice: x: 4, y: 4, z: 8, core: 2. Of those that a mesh axis runs over, the one named last changes fastest.
Arguments:
- tokens: bfloat16 [8192, 2880], P('dp'), may hold values from -14 to 14
- w_query: bfloat16 [2880, 4096], P('dp', 'mp'), may hold values from -0.0559017 to 0.0559017
- w_key: bfloat16 [2880, 512], P('dp', 'mp'), may hold values from -0.0559017 to 0.0559017
- w_value: bfloat16 [2880, 512], P('dp', 'mp'), may hold values from -0.109375 to 0.109375
- w_out: bfloat16 [4096, 2880], P(('mp', 'dp')), may hold values from -0.09375 to 0.09375
- sinks: float32 [64], P('mp'), may hold values from -2 to 2
- grad_out: bfloat16 [8192, 2880], P('dp'), may hold values from -24 to 24
Outputs:
- grad_tokens: bfloat16 [8192, 2880], P('dp', 'mp')
- grad_w_query: float32 [2880, 4096], P('dp', 'mp')
- grad_w_key: float32 [2880, 512], P('dp', 'mp')
- grad_w_value: float32 [2880, 512], P('dp', 'mp')
- grad_w_out: float32 [4096, 2880], P(('mp', 'dp'))
The draws below stay inside these ranges and needn't reach their ends.
All inputs are finite; a program needn't handle non-finite values.
Results may differ from the reference program's by a relative error of at most 0.04.
Values may be sent and summed in bfloat16 or wider, within the bound.
No kernel may reach another device: no remote copies, remote signals or barrier semaphores. Data moves between devices by JAX's collectives and lax.ppermute only.
A program may use at most 64 MiB of HBM per device.

```python
import math
import jax
import jax.numpy as jnp
from jax import lax

D = 2880
HQ = 64
HK = 8
DH = 64
WINDOW = 128
LENGTH = 16384
TOKENS = 8192


def draw_tokens(key, part):
    return jax.random.truncated_normal(jax.random.fold_in(key, 1), -6.0, 6.0, (TOKENS, D), jnp.float32).astype(jnp.bfloat16)


def weight_clip(values):
    limit = 0.996 * 3.0 / math.sqrt(D)
    return jnp.clip(values, -limit, limit).astype(jnp.bfloat16)


def draw_w_query(key, part):
    noise_part = jax.random.truncated_normal(jax.random.fold_in(key, 5), -4.0, 4.0, (D, HQ * DH), jnp.float32) / math.sqrt(D)
    return weight_clip(noise_part)


def draw_w_key(key, part):
    noise_part = jax.random.truncated_normal(jax.random.fold_in(key, 6), -4.0, 4.0, (D, HK * DH), jnp.float32) / math.sqrt(D)
    return weight_clip(noise_part)


def steps_of(stream_key, shape, shards, low, largest):
    gain = 1.0
    for axis_at, blocks in shards:
        draws = jax.random.uniform(jax.random.fold_in(jax.random.fold_in(stream_key, 6), axis_at), (blocks,), jnp.float32, low / len(shards), largest / len(shards))
        gain = gain * jnp.repeat(jnp.exp(draws), shape[axis_at] // blocks).reshape((-1,) + (1,) * (len(shape) - 1 - axis_at))
    return gain


def gaussian(rng, dims, width, most, pieces=(), kind=jnp.bfloat16):
    result = width * jax.random.normal(rng, dims, jnp.float32)
    if pieces:
        result = result * steps_of(rng, dims, pieces, -0.22, 0.18)
    return jnp.clip(result, -most, most).astype(kind)


def setup_inputs(seed: int = 0) -> dict:
    keys = jax.random.split(jax.random.key(seed), 8)
    return {
        "tokens": draw_tokens(jax.random.fold_in(keys[7], 71), 0),
        "w_query": draw_w_query(jax.random.fold_in(keys[7], 71), 0),
        "w_key": draw_w_key(jax.random.fold_in(keys[7], 71), 0),
        "w_value": gaussian(keys[3], (D, HK * DH), D ** -0.5, 0.109375, ((0, 32), (1, 8))),
        "w_out": gaussian(keys[4], (HQ * DH, D), (HQ * DH) ** -0.5, 0.09375, ((0, 256),)),
        "sinks": jnp.clip(jax.random.uniform(keys[5], (HQ,), jnp.float32, -2.0, 2.0) * steps_of(keys[5], (HQ,), ((0, 8),), -0.4, 0.0), -2.0, 2.0),
        "grad_out": gaussian(keys[6], (TOKENS, D), 4.0, 24.0, ((0, 32),)),
    }


masked_score = -1e+30

def contract_rows(left_side, right_side):
    return lax.dot_general(left_side, right_side, (((0,), (0,)), ((), ())), preferred_element_type=jnp.float32)

def contract_cols(left_side, right_side):
    return lax.dot_general(left_side, right_side, (((1,), (1,)), ((), ())), preferred_element_type=jnp.float32)

def band_mask(first_row, blocks, window):
    block_ids = jnp.arange(blocks, dtype=jnp.int32)[:, None, None] * window
    query_pos = first_row + block_ids + jnp.arange(window, dtype=jnp.int32)[None, :, None]
    key_pos = first_row + block_ids + jnp.arange(2 * window, dtype=jnp.int32)[None, None, :] - window
    offset = query_pos - key_pos
    same_resp = jnp.floor_divide(query_pos, LENGTH) == jnp.floor_divide(key_pos, LENGTH)
    return (offset >= 0) & (offset < window) & same_resp

def paired_blocks(extended, window):
    stacked = extended.reshape((-1, window) + extended.shape[1:])
    return jnp.concatenate([stacked[:-1], stacked[1:]], axis=1)

def fold_blocks(paired, window):
    widths = [(0, 0)] * (paired.ndim - 1)
    lower_half = jnp.pad(paired[:, :window], [(0, 1)] + widths)
    upper_half = jnp.pad(paired[:, window:], [(1, 0)] + widths)
    summed = lower_half + upper_half
    return summed.reshape((summed.shape[0] * window,) + summed.shape[2:])

def attend_group(group_item):
    query_grp, key_grp, value_grp, dattn_grp, sink_grp = group_item
    window = WINDOW
    blocks = TOKENS // window
    group_size = query_grp.shape[1]
    score_scale = 1.0 / math.sqrt(DH)
    rim_zeros = jnp.zeros((window, DH), key_grp.dtype)
    key_blk = paired_blocks(jnp.concatenate([rim_zeros, key_grp], axis=0), window)
    value_blk = paired_blocks(jnp.concatenate([rim_zeros, value_grp], axis=0), window)
    query_blk = query_grp.reshape(blocks, window, group_size, DH)
    dattn_blk = dattn_grp.reshape(blocks, window, group_size, DH)
    scores = jnp.einsum('bigd,bjd->bgij', query_blk.astype(jnp.float32), key_blk.astype(jnp.float32)) * score_scale
    allowed = band_mask(0, blocks, window)[:, None]
    scores = jnp.where(allowed, scores, masked_score)
    sink_row = sink_grp.astype(jnp.float32)[None, :, None]
    row_peak = jnp.maximum(lax.optimization_barrier(jnp.max(scores, axis=-1)), sink_row)
    row_total = jnp.exp(sink_row - row_peak) + lax.optimization_barrier(jnp.sum(jnp.exp(scores - row_peak[..., None]), axis=-1))
    log_total = row_peak + jnp.log(row_total)
    prob_full = jnp.exp(scores - log_total[..., None])
    prob_round = prob_full.astype(jnp.bfloat16)
    attended = jnp.einsum('bgij,bjd->bigd', prob_round.astype(jnp.float32), value_blk.astype(jnp.float32)).astype(jnp.bfloat16)
    row_delta = lax.optimization_barrier(jnp.sum(dattn_blk.astype(jnp.float32) * attended.astype(jnp.float32), axis=-1)).transpose(0, 2, 1)
    grad_prob = jnp.einsum('bigd,bjd->bgij', dattn_blk.astype(jnp.float32), value_blk.astype(jnp.float32))
    grad_scores = (prob_full * (grad_prob - row_delta[..., None]) * score_scale).astype(jnp.bfloat16)
    grad_queries = jnp.einsum('bgij,bjd->bigd', grad_scores.astype(jnp.float32), key_blk.astype(jnp.float32)).astype(jnp.bfloat16)
    grad_key_blk = jnp.einsum('bgij,bigd->bjd', grad_scores.astype(jnp.float32), query_blk.astype(jnp.float32))
    grad_value_blk = jnp.einsum('bgij,bigd->bjd', prob_round.astype(jnp.float32), dattn_blk.astype(jnp.float32))
    grad_keys = fold_blocks(grad_key_blk, window)[window:].astype(jnp.bfloat16)
    grad_values = fold_blocks(grad_value_blk, window)[window:].astype(jnp.bfloat16)
    return (attended.reshape(TOKENS, group_size, DH), grad_queries.reshape(TOKENS, group_size, DH), grad_keys, grad_values)

def reference(tokens, w_query, w_key, w_value, w_out, sinks, grad_out):
    group_size = HQ // HK
    queries = jnp.dot(tokens, w_query, preferred_element_type=jnp.float32).astype(jnp.bfloat16)
    key_rows = jnp.dot(tokens, w_key, preferred_element_type=jnp.float32).astype(jnp.bfloat16)
    value_rows = jnp.dot(tokens, w_value, preferred_element_type=jnp.float32).astype(jnp.bfloat16)
    grad_attn = contract_cols(grad_out, w_out).astype(jnp.bfloat16)
    stacked = (queries.reshape(TOKENS, HK, group_size, DH).transpose(1, 0, 2, 3), key_rows.reshape(TOKENS, HK, DH).transpose(1, 0, 2), value_rows.reshape(TOKENS, HK, DH).transpose(1, 0, 2), grad_attn.reshape(TOKENS, HK, group_size, DH).transpose(1, 0, 2, 3), sinks.reshape(HK, group_size))
    attended, grad_queries, grad_keys, grad_values = lax.map(attend_group, stacked)
    attn_rows = attended.transpose(1, 0, 2, 3).reshape(TOKENS, HQ * DH)
    grad_queries = grad_queries.transpose(1, 0, 2, 3).reshape(TOKENS, HQ * DH)
    grad_keys = grad_keys.transpose(1, 0, 2).reshape(TOKENS, HK * DH)
    grad_values = grad_values.transpose(1, 0, 2).reshape(TOKENS, HK * DH)
    grad_tokens = (contract_cols(grad_queries, w_query) + contract_cols(grad_keys, w_key) + contract_cols(grad_values, w_value)).astype(jnp.bfloat16)
    grad_scale = 1.0 / math.sqrt(TOKENS)
    grad_w_query = contract_rows(tokens, grad_queries) * grad_scale
    grad_w_key = contract_rows(tokens, grad_keys) * grad_scale
    grad_w_value = contract_rows(tokens, grad_values) * grad_scale
    grad_w_out = contract_rows(attn_rows, grad_out) * grad_scale
    return (grad_tokens, grad_w_query, grad_w_key, grad_w_value, grad_w_out)
```

```python
import math

import jax
import jax.numpy as jnp
from jax import lax
from jax.sharding import Mesh, PartitionSpec as P

DH = 64
WINDOW = 128
LENGTH = 16384


masked_score = -1e30
DP_AXES = ("dx", "dz")
LANES = 128


def passed_along(array, axis, by):
    peers = lax.axis_size(axis)
    pairs = [(i, i + by) for i in range(peers) if 0 <= i + by < peers]
    return lax.ppermute(array, axis, pairs)


def contract_rows(left_side, right_side):
    return lax.dot_general(
        left_side, right_side, (((0,), (0,)), ((), ())), preferred_element_type=jnp.float32
    )


def contract_cols(left_side, right_side):
    return lax.dot_general(
        left_side, right_side, (((1,), (1,)), ((), ())), preferred_element_type=jnp.float32
    )


def band_mask(first_row, blocks, window):
    block_ids = jnp.arange(blocks, dtype=jnp.int32)[:, None, None] * window
    query_pos = first_row + block_ids + jnp.arange(window, dtype=jnp.int32)[None, :, None]
    key_pos = (
        first_row + block_ids + jnp.arange(2 * window, dtype=jnp.int32)[None, None, :] - window
    )
    offset = query_pos - key_pos
    same_resp = jnp.floor_divide(query_pos, LENGTH) == jnp.floor_divide(key_pos, LENGTH)
    return (offset >= 0) & (offset < window) & same_resp


def paired_blocks(extended, window):
    stacked = extended.reshape((-1, window) + extended.shape[1:])
    return jnp.concatenate([stacked[:-1], stacked[1:]], axis=1)


def fold_blocks(paired, window):
    widths = [(0, 0)] * (paired.ndim - 1)
    lower_half = jnp.pad(paired[:, :window], [(0, 1)] + widths)
    upper_half = jnp.pad(paired[:, window:], [(1, 0)] + widths)
    summed = lower_half + upper_half
    return summed.reshape((summed.shape[0] * window,) + summed.shape[2:])


def gather_weights(w_query, w_key, w_value, w_out):
    pieces = (w_query, w_key, w_value, w_out)
    flat = jnp.concatenate([p.reshape(-1) for p in pieces])
    gathered = lax.all_gather(flat.reshape(1, -1, LANES), DP_AXES, axis=0, tiled=True)
    peers = gathered.shape[0]
    gathered = gathered.reshape(peers, -1)
    full = []
    at = 0
    for p in pieces:
        size = p.size
        part = gathered[:, at : at + size].reshape((peers * p.shape[0],) + p.shape[1:])
        full.append(part)
        at += size
    return full


def scatter_weight_grads(partials, x_peers, z_peers):
    rows = []
    for p in partials:
        blocked = p.astype(jnp.bfloat16).reshape(x_peers, z_peers, -1)
        rows.append(jnp.swapaxes(blocked, 0, 1))
    packed = jnp.concatenate(rows, axis=-1)
    packed = packed.reshape(z_peers, x_peers, -1, LANES)
    over_z = lax.psum_scatter(packed, "dz", scatter_dimension=0, tiled=True)[0]
    over_x = lax.psum_scatter(over_z, "dx", scatter_dimension=0, tiled=True)[0]
    over_x = over_x.reshape(-1)
    out = []
    at = 0
    for p in partials:
        size = p.size // (x_peers * z_peers)
        shape = (p.shape[0] // (x_peers * z_peers),) + p.shape[1:]
        out.append(over_x[at : at + size].astype(jnp.float32).reshape(shape))
        at += size
    return out


def scatter_cols_mp(terms):
    peers = lax.axis_size("mp")
    me = lax.axis_index("mp")
    width = terms.shape[1] // peers
    blocks = terms.reshape(terms.shape[0], peers, width)
    total = lax.dynamic_index_in_dim(blocks, me, axis=1, keepdims=False)
    for shift in range(1, peers):
        dest = (me + shift) % peers
        piece = lax.dynamic_index_in_dim(blocks, dest, axis=1, keepdims=False)
        pairs = [(i, (i + shift) % peers) for i in range(peers)]
        got = lax.ppermute(piece.astype(jnp.bfloat16), "mp", pairs)
        total = total + got.astype(jnp.float32)
    return total.astype(jnp.bfloat16)


def shards(tokens, w_query, w_key, w_value, w_out, sinks, grad_out):
    row_count = tokens.shape[0]
    window = WINDOW
    blocks = row_count // window
    score_scale = 1.0 / math.sqrt(DH)
    x_peers = lax.axis_size("dx")
    z_peers = lax.axis_size("dz")
    full_query, full_key, full_value, full_out = gather_weights(w_query, w_key, w_value, w_out)
    kv_heads = full_key.shape[1] // DH
    group_size = full_query.shape[1] // DH // kv_heads
    queries = jnp.dot(tokens, full_query, preferred_element_type=jnp.float32).astype(jnp.bfloat16)
    key_rows = jnp.dot(tokens, full_key, preferred_element_type=jnp.float32).astype(jnp.bfloat16)
    value_rows = jnp.dot(tokens, full_value, preferred_element_type=jnp.float32).astype(
        jnp.bfloat16
    )
    rim_keys, rim_values = passed_along((key_rows[-window:], value_rows[-window:]), DP_AXES, 1)
    grad_attn = contract_cols(grad_out, full_out).astype(jnp.bfloat16)
    first_row = (lax.axis_index("dx") * z_peers + lax.axis_index("dz")) * row_count
    ext_keys = jnp.concatenate([rim_keys, key_rows], axis=0).reshape(
        row_count + window, kv_heads, DH
    )
    ext_values = jnp.concatenate([rim_values, value_rows], axis=0).reshape(
        row_count + window, kv_heads, DH
    )
    key_blk = paired_blocks(ext_keys, window)
    value_blk = paired_blocks(ext_values, window)
    query_blk = queries.reshape(blocks, window, kv_heads, group_size, DH)
    dattn_blk = grad_attn.reshape(blocks, window, kv_heads, group_size, DH)
    scores = (
        jnp.einsum("bikgd,bjkd->bkgij", query_blk, key_blk, preferred_element_type=jnp.float32)
        * score_scale
    )
    allowed = band_mask(first_row, blocks, window)[:, None, None]
    scores = jnp.where(allowed, scores, masked_score)
    sink_row = sinks.reshape(kv_heads, group_size)[None, :, :, None]
    row_peak = jnp.maximum(jnp.max(scores, axis=-1), sink_row)
    row_total = jnp.exp(sink_row - row_peak) + jnp.sum(
        jnp.exp(scores - row_peak[..., None]), axis=-1
    )
    log_total = row_peak + jnp.log(row_total)
    prob_full = jnp.exp(scores - log_total[..., None])
    prob_round = prob_full.astype(jnp.bfloat16)
    attended = jnp.einsum(
        "bkgij,bjkd->bikgd", prob_round, value_blk, preferred_element_type=jnp.float32
    ).astype(jnp.bfloat16)
    attn_rows = attended.reshape(row_count, -1)
    grad_out_w = contract_rows(attn_rows, grad_out)
    row_delta = jnp.sum(
        dattn_blk.astype(jnp.float32) * attended.astype(jnp.float32), axis=-1
    ).transpose(0, 2, 3, 1)
    grad_prob = jnp.einsum(
        "bikgd,bjkd->bkgij", dattn_blk, value_blk, preferred_element_type=jnp.float32
    )
    grad_scores = (prob_full * (grad_prob - row_delta[..., None]) * score_scale).astype(
        jnp.bfloat16
    )
    grad_queries = (
        jnp.einsum("bkgij,bjkd->bikgd", grad_scores, key_blk, preferred_element_type=jnp.float32)
        .astype(jnp.bfloat16)
        .reshape(row_count, -1)
    )
    grad_key_blk = jnp.einsum(
        "bkgij,bikgd->bjkd", grad_scores, query_blk, preferred_element_type=jnp.float32
    )
    grad_value_blk = jnp.einsum(
        "bkgij,bikgd->bjkd", prob_round, dattn_blk, preferred_element_type=jnp.float32
    )
    grad_key_ext = fold_blocks(grad_key_blk, window).reshape(row_count + window, -1)
    grad_value_ext = fold_blocks(grad_value_blk, window).reshape(row_count + window, -1)
    back_keys, back_values = (
        passed_along(grad_key_ext[:window].astype(jnp.bfloat16), DP_AXES, -1).astype(jnp.float32),
        passed_along(grad_value_ext[:window].astype(jnp.bfloat16), DP_AXES, -1).astype(jnp.float32),
    )
    own_keys = grad_key_ext[window:]
    own_values = grad_value_ext[window:]
    grad_keys = jnp.concatenate(
        [own_keys[:-window], own_keys[-window:] + back_keys], axis=0
    ).astype(jnp.bfloat16)
    grad_values = jnp.concatenate(
        [own_values[:-window], own_values[-window:] + back_values], axis=0
    ).astype(jnp.bfloat16)
    token_terms = (
        contract_cols(grad_queries, full_query)
        + contract_cols(grad_keys, full_key)
        + contract_cols(grad_values, full_value)
    )
    grad_tokens = scatter_cols_mp(token_terms)
    grad_q_term = contract_rows(tokens, grad_queries)
    grad_k_term = contract_rows(tokens, grad_keys)
    grad_v_term = contract_rows(tokens, grad_values)
    summed_q, summed_k, summed_v, summed_out = scatter_weight_grads(
        (grad_q_term, grad_k_term, grad_v_term, grad_out_w), x_peers, z_peers
    )
    grad_scale = 1.0 / math.sqrt(row_count * x_peers * z_peers)
    return (
        grad_tokens,
        summed_q * grad_scale,
        summed_k * grad_scale,
        summed_v * grad_scale,
        summed_out * grad_scale,
    )


def split_mesh(mesh):
    dp = mesh.shape["dp"]
    try:
        x_peers = len({d.coords[0] for d in mesh.devices.flat})
    except AttributeError:
        x_peers = 4
    if dp % x_peers:
        x_peers = 1
    devices = mesh.devices.reshape(x_peers, dp // x_peers, mesh.shape["mp"])
    return Mesh(devices, ("dx", "dz", "mp"))


def solution(mesh):
    mesh = split_mesh(mesh)
    dp = DP_AXES
    return jax.shard_map(
        shards,
        mesh=mesh,
        in_specs=(
            P(dp, None),
            P(dp, "mp"),
            P(dp, "mp"),
            P(dp, "mp"),
            P(("mp",) + dp, None),
            P("mp"),
            P(dp, None),
        ),
        out_specs=(
            P(dp, "mp"),
            P(dp, "mp"),
            P(dp, "mp"),
            P(dp, "mp"),
            P(("mp",) + dp, None),
        ),
        check_vma=False,
    )
```

```python
import math

import jax
import jax.numpy as jnp
from jax import lax
from jax.sharding import Mesh, PartitionSpec as P

DH = 64
WINDOW = 128
LENGTH = 16384


masked_score = -1e30
DP_AXES = ("dx", "dz")
LANES = 128


def passed_along(array, axis, by):
    peers = lax.axis_size(axis)
    pairs = [(i, i + by) for i in range(peers) if 0 <= i + by < peers]
    return lax.ppermute(array, axis, pairs)


def contract_rows(left_side, right_side):
    return lax.dot_general(
        left_side, right_side, (((0,), (0,)), ((), ())), preferred_element_type=jnp.float32
    )


def contract_cols(left_side, right_side):
    return lax.dot_general(
        left_side, right_side, (((1,), (1,)), ((), ())), preferred_element_type=jnp.float32
    )


def band_mask(first_row, blocks, window):
    block_ids = jnp.arange(blocks, dtype=jnp.int32)[:, None, None] * window
    query_pos = first_row + block_ids + jnp.arange(window, dtype=jnp.int32)[None, :, None]
    key_pos = (
        first_row + block_ids + jnp.arange(2 * window, dtype=jnp.int32)[None, None, :] - window
    )
    offset = query_pos - key_pos
    same_resp = jnp.floor_divide(query_pos, LENGTH) == jnp.floor_divide(key_pos, LENGTH)
    return (offset >= 0) & (offset < window) & same_resp


def paired_blocks(extended, window):
    stacked = extended.reshape((-1, window) + extended.shape[1:])
    return jnp.concatenate([stacked[:-1], stacked[1:]], axis=1)


def fold_blocks(paired, window):
    widths = [(0, 0)] * (paired.ndim - 1)
    lower_half = jnp.pad(paired[:, :window], [(0, 1)] + widths)
    upper_half = jnp.pad(paired[:, window:], [(1, 0)] + widths)
    summed = lower_half + upper_half
    return summed.reshape((summed.shape[0] * window,) + summed.shape[2:])


def rows_of(array, lead):
    return array.reshape(array.shape[:1] + lead + (-1,))


def scatter_cols_mp(terms):
    peers = lax.axis_size("mp")
    me = lax.axis_index("mp")
    total = lax.dynamic_index_in_dim(terms, me, axis=1, keepdims=False)
    for shift in range(1, peers):
        dest = (me + shift) % peers
        piece = lax.dynamic_index_in_dim(terms, dest, axis=1, keepdims=False)
        pairs = [(i, (i + shift) % peers) for i in range(peers)]
        got = lax.ppermute(piece.astype(jnp.bfloat16), "mp", pairs)
        total = total + got.astype(jnp.float32)
    return total.reshape(total.shape[0], -1).astype(jnp.bfloat16)


def contract_by_z(left_side, right_side, x_peers, z_peers):
    by_z = left_side.reshape(left_side.shape[0], x_peers, z_peers, -1).transpose(0, 2, 1, 3)
    by_z = by_z.reshape(left_side.shape[0], z_peers, -1)
    return jnp.einsum(
        "tzq,tc->zqc", by_z, right_side, preferred_element_type=jnp.float32
    ).astype(jnp.bfloat16)


def scatter_rows_dp(part, x_peers):
    over_z = lax.psum_scatter(part, "dz", scatter_dimension=0, tiled=True)[0]
    over_z = over_z.reshape((x_peers, -1) + over_z.shape[1:])
    over_x = lax.psum_scatter(over_z, "dx", scatter_dimension=0, tiled=True)[0]
    return over_x.astype(jnp.float32)


def shards(tokens, w_query, w_key, w_value, w_out, sinks, grad_out):
    row_count = tokens.shape[0]
    window = WINDOW
    blocks = row_count // window
    score_scale = 1.0 / math.sqrt(DH)
    x_peers = lax.axis_size("dx")
    z_peers = lax.axis_size("dz")
    mp_peers = lax.axis_size("mp")
    dp_peers = x_peers * z_peers
    q_cols, k_cols, v_cols = w_query.shape[1], w_key.shape[1], w_value.shape[1]
    in_proj = jnp.concatenate([w_query, w_key, w_value], axis=1)
    in_full, out_full = lax.all_gather((in_proj, w_out), DP_AXES, axis=0, tiled=False)
    full_out = out_full.reshape((-1,) + out_full.shape[2:])
    kv_heads = k_cols // DH
    group_size = q_cols // DH // kv_heads
    tokens_blk = rows_of(tokens, (dp_peers,))
    qkv = jnp.einsum("tdr,drc->tc", tokens_blk, in_full, preferred_element_type=jnp.float32).astype(
        jnp.bfloat16
    )
    queries = qkv[:, :q_cols]
    key_rows = qkv[:, q_cols : q_cols + k_cols]
    value_rows = qkv[:, q_cols + k_cols :]
    rim_keys, rim_values = passed_along((key_rows[-window:], value_rows[-window:]), DP_AXES, 1)
    grad_attn = contract_cols(grad_out, full_out).astype(jnp.bfloat16)
    first_row = (lax.axis_index("dx") * z_peers + lax.axis_index("dz")) * row_count
    ext_keys = jnp.concatenate([rim_keys, key_rows], axis=0).reshape(
        row_count + window, kv_heads, DH
    )
    ext_values = jnp.concatenate([rim_values, value_rows], axis=0).reshape(
        row_count + window, kv_heads, DH
    )
    key_blk = paired_blocks(ext_keys, window)
    value_blk = paired_blocks(ext_values, window)
    query_blk = queries.reshape(blocks, window, kv_heads, group_size, DH)
    dattn_blk = grad_attn.reshape(blocks, window, kv_heads, group_size, DH)
    scores = (
        jnp.einsum("bikgd,bjkd->bkgij", query_blk, key_blk, preferred_element_type=jnp.float32)
        * score_scale
    )
    allowed = band_mask(first_row, blocks, window)[:, None, None]
    scores = jnp.where(allowed, scores, masked_score)
    sink_row = sinks.reshape(kv_heads, group_size)[None, :, :, None]
    row_peak = jnp.maximum(jnp.max(scores, axis=-1), sink_row)
    row_total = jnp.exp(sink_row - row_peak) + jnp.sum(
        jnp.exp(scores - row_peak[..., None]), axis=-1
    )
    log_total = row_peak + jnp.log(row_total)
    prob_full = jnp.exp(scores - log_total[..., None])
    prob_round = prob_full.astype(jnp.bfloat16)
    attended = jnp.einsum(
        "bkgij,bjkd->bikgd", prob_round, value_blk, preferred_element_type=jnp.float32
    ).astype(jnp.bfloat16)
    attn_rows = attended.reshape(row_count, -1)
    row_delta = jnp.sum(
        dattn_blk.astype(jnp.float32) * attended.astype(jnp.float32), axis=-1
    ).transpose(0, 2, 3, 1)
    grad_prob = jnp.einsum(
        "bikgd,bjkd->bkgij", dattn_blk, value_blk, preferred_element_type=jnp.float32
    )
    grad_scores = (prob_full * (grad_prob - row_delta[..., None]) * score_scale).astype(
        jnp.bfloat16
    )
    grad_queries = (
        jnp.einsum("bkgij,bjkd->bikgd", grad_scores, key_blk, preferred_element_type=jnp.float32)
        .astype(jnp.bfloat16)
        .reshape(row_count, -1)
    )
    grad_key_blk = jnp.einsum(
        "bkgij,bikgd->bjkd", grad_scores, query_blk, preferred_element_type=jnp.float32
    )
    grad_value_blk = jnp.einsum(
        "bkgij,bikgd->bjkd", prob_round, dattn_blk, preferred_element_type=jnp.float32
    )
    grad_key_ext = fold_blocks(grad_key_blk, window).reshape(row_count + window, -1)
    grad_value_ext = fold_blocks(grad_value_blk, window).reshape(row_count + window, -1)
    back_keys, back_values = (
        passed_along(grad_key_ext[:window].astype(jnp.bfloat16), DP_AXES, -1).astype(jnp.float32),
        passed_along(grad_value_ext[:window].astype(jnp.bfloat16), DP_AXES, -1).astype(jnp.float32),
    )
    own_keys = grad_key_ext[window:]
    own_values = grad_value_ext[window:]
    grad_keys = jnp.concatenate(
        [own_keys[:-window], own_keys[-window:] + back_keys], axis=0
    ).astype(jnp.bfloat16)
    grad_values = jnp.concatenate(
        [own_values[:-window], own_values[-window:] + back_values], axis=0
    ).astype(jnp.bfloat16)
    grad_qkv = jnp.concatenate([grad_queries, grad_keys, grad_values], axis=1)
    proj_by_mp = in_full.reshape((mp_peers, -1) + in_full.shape[1:])
    token_terms = jnp.einsum(
        "tc,mjrc->tmjr", grad_qkv, proj_by_mp, preferred_element_type=jnp.float32
    )
    grad_tokens = scatter_cols_mp(token_terms)
    grad_in = scatter_rows_dp(contract_by_z(tokens, grad_qkv, x_peers, z_peers), x_peers)
    grad_w_out = scatter_rows_dp(contract_by_z(attn_rows, grad_out, x_peers, z_peers), x_peers)
    grad_scale = 1.0 / math.sqrt(row_count * dp_peers)
    grad_in = grad_in * grad_scale
    return (
        grad_tokens,
        grad_in[:, :q_cols],
        grad_in[:, q_cols : q_cols + k_cols],
        grad_in[:, q_cols + k_cols :],
        grad_w_out * grad_scale,
    )


def split_mesh(mesh):
    dp = mesh.shape["dp"]
    try:
        x_peers = len({d.coords[0] for d in mesh.devices.flat})
    except AttributeError:
        x_peers = 4
    if dp % x_peers:
        x_peers = 1
    devices = mesh.devices.reshape(x_peers, dp // x_peers, mesh.shape["mp"])
    return Mesh(devices, ("dx", "dz", "mp"))


def solution(mesh):
    mesh = split_mesh(mesh)
    dp = DP_AXES
    return jax.shard_map(
        shards,
        mesh=mesh,
        in_specs=(
            P(dp, None),
            P(dp, "mp"),
            P(dp, "mp"),
            P(dp, "mp"),
            P(("mp",) + dp, None),
            P("mp"),
            P(dp, None),
        ),
        out_specs=(
            P(dp, "mp"),
            P(dp, "mp"),
            P(dp, "mp"),
            P(dp, "mp"),
            P(("mp",) + dp, None),
        ),
        check_vma=False,
    )
```

```python
import math

import jax
import jax.numpy as jnp
from jax import lax
from jax.sharding import Mesh, PartitionSpec as P

DH = 64
WINDOW = 128
LENGTH = 16384


masked_score = -1e30
DP_AXES = ("dx", "dz")
LANES = 128


def passed_along(array, axis, by):
    peers = lax.axis_size(axis)
    pairs = [(i, i + by) for i in range(peers) if 0 <= i + by < peers]
    return lax.ppermute(array, axis, pairs)


def contract_rows(left_side, right_side):
    return lax.dot_general(
        left_side, right_side, (((0,), (0,)), ((), ())), preferred_element_type=jnp.float32
    )


def contract_cols(left_side, right_side):
    return lax.dot_general(
        left_side, right_side, (((1,), (1,)), ((), ())), preferred_element_type=jnp.float32
    )


def band_mask(first_row, blocks, window):
    block_ids = jnp.arange(blocks, dtype=jnp.int32)[:, None, None] * window
    query_pos = first_row + block_ids + jnp.arange(window, dtype=jnp.int32)[None, :, None]
    key_pos = (
        first_row + block_ids + jnp.arange(2 * window, dtype=jnp.int32)[None, None, :] - window
    )
    offset = query_pos - key_pos
    same_resp = jnp.floor_divide(query_pos, LENGTH) == jnp.floor_divide(key_pos, LENGTH)
    return (offset >= 0) & (offset < window) & same_resp


def paired_blocks(extended, window):
    stacked = extended.reshape((-1, window) + extended.shape[1:])
    return jnp.concatenate([stacked[:-1], stacked[1:]], axis=1)


def fold_blocks(paired, window):
    widths = [(0, 0)] * (paired.ndim - 1)
    lower_half = jnp.pad(paired[:, :window], [(0, 1)] + widths)
    upper_half = jnp.pad(paired[:, window:], [(1, 0)] + widths)
    summed = lower_half + upper_half
    return summed.reshape((summed.shape[0] * window,) + summed.shape[2:])


def rows_of(array, lead):
    return array.reshape(array.shape[:1] + lead + (-1,))


def scatter_cols_mp(terms):
    peers = lax.axis_size("mp")
    me = lax.axis_index("mp")
    total = lax.dynamic_index_in_dim(terms, me, axis=1, keepdims=False)
    for shift in range(1, peers):
        dest = (me + shift) % peers
        piece = lax.dynamic_index_in_dim(terms, dest, axis=1, keepdims=False)
        pairs = [(i, (i + shift) % peers) for i in range(peers)]
        got = lax.ppermute(piece.astype(jnp.bfloat16), "mp", pairs)
        total = total + got.astype(jnp.float32)
    return total.reshape(total.shape[0], -1).astype(jnp.bfloat16)


def by_zx(rows, x_peers, z_peers):
    split = rows.reshape(rows.shape[0], x_peers, z_peers, -1)
    return split.transpose(0, 2, 1, 3)


def shards(tokens, w_query, w_key, w_value, w_out, sinks, grad_out):
    row_count = tokens.shape[0]
    window = WINDOW
    blocks = row_count // window
    score_scale = 1.0 / math.sqrt(DH)
    x_peers = lax.axis_size("dx")
    z_peers = lax.axis_size("dz")
    mp_peers = lax.axis_size("mp")
    dp_peers = x_peers * z_peers
    q_cols, k_cols, v_cols = w_query.shape[1], w_key.shape[1], w_value.shape[1]
    in_width = q_cols + k_cols + v_cols
    out_rows = w_out.shape[0]
    packed = jnp.concatenate(
        [w_query, w_key, w_value, w_out.reshape(w_query.shape[0], -1)], axis=1
    )
    gathered = lax.all_gather(packed, DP_AXES, axis=0, tiled=False)
    in_full = gathered[:, :, :in_width]
    full_out = gathered[:, :, in_width:].reshape((-1,) + w_out.shape[1:])
    kv_heads = k_cols // DH
    group_size = q_cols // DH // kv_heads
    tokens_blk = rows_of(tokens, (dp_peers,))
    qkv = jnp.einsum("tdr,drc->tc", tokens_blk, in_full, preferred_element_type=jnp.float32).astype(
        jnp.bfloat16
    )
    queries = qkv[:, :q_cols]
    key_rows = qkv[:, q_cols : q_cols + k_cols]
    value_rows = qkv[:, q_cols + k_cols :]
    rim_keys, rim_values = passed_along((key_rows[-window:], value_rows[-window:]), DP_AXES, 1)
    grad_attn = contract_cols(grad_out, full_out).astype(jnp.bfloat16)
    first_row = (lax.axis_index("dx") * z_peers + lax.axis_index("dz")) * row_count
    ext_keys = jnp.concatenate([rim_keys, key_rows], axis=0).reshape(
        row_count + window, kv_heads, DH
    )
    ext_values = jnp.concatenate([rim_values, value_rows], axis=0).reshape(
        row_count + window, kv_heads, DH
    )
    key_blk = paired_blocks(ext_keys, window)
    value_blk = paired_blocks(ext_values, window)
    query_blk = queries.reshape(blocks, window, kv_heads, group_size, DH)
    dattn_blk = grad_attn.reshape(blocks, window, kv_heads, group_size, DH)
    scores = (
        jnp.einsum("bikgd,bjkd->bkgij", query_blk, key_blk, preferred_element_type=jnp.float32)
        * score_scale
    )
    allowed = band_mask(first_row, blocks, window)[:, None, None]
    scores = jnp.where(allowed, scores, masked_score)
    sink_row = sinks.reshape(kv_heads, group_size)[None, :, :, None]
    row_peak = jnp.maximum(jnp.max(scores, axis=-1), sink_row)
    row_total = jnp.exp(sink_row - row_peak) + jnp.sum(
        jnp.exp(scores - row_peak[..., None]), axis=-1
    )
    log_total = row_peak + jnp.log(row_total)
    prob_full = jnp.exp(scores - log_total[..., None])
    prob_round = prob_full.astype(jnp.bfloat16)
    attended = jnp.einsum(
        "bkgij,bjkd->bikgd", prob_round, value_blk, preferred_element_type=jnp.float32
    ).astype(jnp.bfloat16)
    attn_rows = attended.reshape(row_count, -1)
    row_delta = jnp.sum(
        dattn_blk.astype(jnp.float32) * attended.astype(jnp.float32), axis=-1
    ).transpose(0, 2, 3, 1)
    grad_prob = jnp.einsum(
        "bikgd,bjkd->bkgij", dattn_blk, value_blk, preferred_element_type=jnp.float32
    )
    grad_scores = (prob_full * (grad_prob - row_delta[..., None]) * score_scale).astype(
        jnp.bfloat16
    )
    grad_queries = (
        jnp.einsum("bkgij,bjkd->bikgd", grad_scores, key_blk, preferred_element_type=jnp.float32)
        .astype(jnp.bfloat16)
        .reshape(row_count, -1)
    )
    grad_key_blk = jnp.einsum(
        "bkgij,bikgd->bjkd", grad_scores, query_blk, preferred_element_type=jnp.float32
    )
    grad_value_blk = jnp.einsum(
        "bkgij,bikgd->bjkd", prob_round, dattn_blk, preferred_element_type=jnp.float32
    )
    grad_key_ext = fold_blocks(grad_key_blk, window).reshape(row_count + window, -1)
    grad_value_ext = fold_blocks(grad_value_blk, window).reshape(row_count + window, -1)
    back_keys, back_values = (
        passed_along(grad_key_ext[:window].astype(jnp.bfloat16), DP_AXES, -1).astype(jnp.float32),
        passed_along(grad_value_ext[:window].astype(jnp.bfloat16), DP_AXES, -1).astype(jnp.float32),
    )
    own_keys = grad_key_ext[window:]
    own_values = grad_value_ext[window:]
    grad_keys = jnp.concatenate(
        [own_keys[:-window], own_keys[-window:] + back_keys], axis=0
    ).astype(jnp.bfloat16)
    grad_values = jnp.concatenate(
        [own_values[:-window], own_values[-window:] + back_values], axis=0
    ).astype(jnp.bfloat16)
    grad_qkv = jnp.concatenate([grad_queries, grad_keys, grad_values], axis=1)
    proj_by_mp = in_full.reshape((mp_peers, -1) + in_full.shape[1:])
    token_terms = jnp.einsum(
        "tc,mjrc->tmjr", grad_qkv, proj_by_mp, preferred_element_type=jnp.float32
    )
    grad_tokens = scatter_cols_mp(token_terms)
    tokens_zx = by_zx(tokens, x_peers, z_peers)
    grad_in_part = jnp.einsum(
        "tzxr,tc->zxrc", tokens_zx, grad_qkv, preferred_element_type=jnp.float32
    ).astype(jnp.bfloat16)
    attn_zx = by_zx(attn_rows, x_peers, z_peers)
    grad_out_part = jnp.einsum(
        "tzxi,tc->zxic", attn_zx, grad_out, preferred_element_type=jnp.float32
    ).astype(jnp.bfloat16)
    grad_out_part = grad_out_part.reshape(z_peers, x_peers, -1, in_width)
    both = jnp.concatenate([grad_in_part, grad_out_part], axis=2)
    over_z = lax.psum_scatter(both, "dz", scatter_dimension=0, tiled=True)[0]
    over_x = lax.psum_scatter(over_z, "dx", scatter_dimension=0, tiled=True)[0].astype(jnp.float32)
    in_rows = w_query.shape[0]
    grad_in = over_x[:in_rows]
    grad_w_out = over_x[in_rows:].reshape(w_out.shape)
    grad_scale = 1.0 / math.sqrt(row_count * dp_peers)
    grad_in = grad_in * grad_scale
    return (
        grad_tokens,
        grad_in[:, :q_cols],
        grad_in[:, q_cols : q_cols + k_cols],
        grad_in[:, q_cols + k_cols :],
        grad_w_out * grad_scale,
    )


def split_mesh(mesh):
    dp = mesh.shape["dp"]
    try:
        x_peers = len({d.coords[0] for d in mesh.devices.flat})
    except AttributeError:
        x_peers = 4
    if dp % x_peers:
        x_peers = 1
    devices = mesh.devices.reshape(x_peers, dp // x_peers, mesh.shape["mp"])
    return Mesh(devices, ("dx", "dz", "mp"))


def solution(mesh):
    mesh = split_mesh(mesh)
    dp = DP_AXES
    return jax.shard_map(
        shards,
        mesh=mesh,
        in_specs=(
            P(dp, None),
            P(dp, "mp"),
            P(dp, "mp"),
            P(dp, "mp"),
            P(("mp",) + dp, None),
            P("mp"),
            P(dp, None),
        ),
        out_specs=(
            P(dp, "mp"),
            P(dp, "mp"),
            P(dp, "mp"),
            P(dp, "mp"),
            P(("mp",) + dp, None),
        ),
        check_vma=False,
    )
```

```python
import math

import jax
import jax.numpy as jnp
from jax import lax
from jax.sharding import Mesh, PartitionSpec as P

DH = 64
WINDOW = 128
LENGTH = 16384


masked_score = -1e30
DP_AXES = ("dx", "dz")
LANES = 128


def passed_along(array, axis, by):
    peers = lax.axis_size(axis)
    pairs = [(i, i + by) for i in range(peers) if 0 <= i + by < peers]
    return lax.ppermute(array, axis, pairs)


def contract_rows(left_side, right_side):
    return lax.dot_general(
        left_side, right_side, (((0,), (0,)), ((), ())), preferred_element_type=jnp.float32
    )


def contract_cols(left_side, right_side):
    return lax.dot_general(
        left_side, right_side, (((1,), (1,)), ((), ())), preferred_element_type=jnp.float32
    )


def band_mask(first_row, blocks, window):
    block_ids = jnp.arange(blocks, dtype=jnp.int32)[:, None, None] * window
    query_pos = first_row + block_ids + jnp.arange(window, dtype=jnp.int32)[None, :, None]
    key_pos = (
        first_row + block_ids + jnp.arange(2 * window, dtype=jnp.int32)[None, None, :] - window
    )
    offset = query_pos - key_pos
    same_resp = jnp.floor_divide(query_pos, LENGTH) == jnp.floor_divide(key_pos, LENGTH)
    return (offset >= 0) & (offset < window) & same_resp


def paired_blocks(extended, window):
    stacked = extended.reshape((-1, window) + extended.shape[1:])
    return jnp.concatenate([stacked[:-1], stacked[1:]], axis=1)


def fold_blocks(paired, window):
    widths = [(0, 0)] * (paired.ndim - 1)
    lower_half = jnp.pad(paired[:, :window], [(0, 1)] + widths)
    upper_half = jnp.pad(paired[:, window:], [(1, 0)] + widths)
    summed = lower_half + upper_half
    return summed.reshape((summed.shape[0] * window,) + summed.shape[2:])


def rows_of(array, lead):
    return array.reshape(array.shape[:1] + lead + (-1,))


def scatter_cols_mp(terms):
    peers = lax.axis_size("mp")
    me = lax.axis_index("mp")
    total = lax.dynamic_index_in_dim(terms, me, axis=1, keepdims=False)
    for shift in range(1, peers):
        dest = (me + shift) % peers
        piece = lax.dynamic_index_in_dim(terms, dest, axis=1, keepdims=False)
        pairs = [(i, (i + shift) % peers) for i in range(peers)]
        got = lax.ppermute(piece.astype(jnp.bfloat16), "mp", pairs)
        total = total + got.astype(jnp.float32)
    return total.reshape(total.shape[0], -1).astype(jnp.bfloat16)


def by_zx(rows, x_peers, z_peers):
    split = rows.reshape(rows.shape[0], x_peers, z_peers, -1)
    return split.transpose(0, 2, 1, 3)


def shards(tokens, w_query, w_key, w_value, w_out, sinks, grad_out):
    row_count = tokens.shape[0]
    window = WINDOW
    blocks = row_count // window
    score_scale = 1.0 / math.sqrt(DH)
    x_peers = lax.axis_size("dx")
    z_peers = lax.axis_size("dz")
    mp_peers = lax.axis_size("mp")
    dp_peers = x_peers * z_peers
    q_cols, k_cols, v_cols = w_query.shape[1], w_key.shape[1], w_value.shape[1]
    in_width = q_cols + k_cols + v_cols
    out_rows = w_out.shape[0]
    packed = jnp.concatenate(
        [w_query, w_key, w_value, w_out.reshape(w_query.shape[0], -1)], axis=1
    )
    gathered = lax.all_gather(packed, DP_AXES, axis=0, tiled=False)
    in_full = gathered[:, :, :in_width]
    full_out = gathered[:, :, in_width:].reshape((-1,) + w_out.shape[1:])
    kv_heads = k_cols // DH
    group_size = q_cols // DH // kv_heads
    tokens_blk = rows_of(tokens, (dp_peers,))
    qkv = jnp.einsum("tdr,drc->tc", tokens_blk, in_full, preferred_element_type=jnp.float32).astype(
        jnp.bfloat16
    )
    queries = qkv[:, :q_cols]
    key_rows = qkv[:, q_cols : q_cols + k_cols]
    value_rows = qkv[:, q_cols + k_cols :]
    rim_keys, rim_values = passed_along((key_rows[-window:], value_rows[-window:]), DP_AXES, 1)
    grad_attn = contract_cols(grad_out, full_out).astype(jnp.bfloat16)
    first_row = (lax.axis_index("dx") * z_peers + lax.axis_index("dz")) * row_count
    ext_keys = jnp.concatenate([rim_keys, key_rows], axis=0).reshape(
        row_count + window, kv_heads, DH
    )
    ext_values = jnp.concatenate([rim_values, value_rows], axis=0).reshape(
        row_count + window, kv_heads, DH
    )
    key_blk = paired_blocks(ext_keys, window)
    value_blk = paired_blocks(ext_values, window)
    query_blk = queries.reshape(blocks, window, kv_heads, group_size, DH)
    dattn_blk = grad_attn.reshape(blocks, window, kv_heads, group_size, DH)
    scores = (
        jnp.einsum("bikgd,bjkd->bkgij", query_blk, key_blk, preferred_element_type=jnp.float32)
        * score_scale
    )
    allowed = band_mask(first_row, blocks, window)[:, None, None]
    scores = jnp.where(allowed, scores, masked_score)
    sink_row = sinks.reshape(kv_heads, group_size)[None, :, :, None]
    row_peak = jnp.maximum(jnp.max(scores, axis=-1), sink_row)
    row_total = jnp.exp(sink_row - row_peak) + jnp.sum(
        jnp.exp(scores - row_peak[..., None]), axis=-1
    )
    log_total = row_peak + jnp.log(row_total)
    prob_full = jnp.exp(scores - log_total[..., None])
    prob_round = prob_full.astype(jnp.bfloat16)
    attended = jnp.einsum(
        "bkgij,bjkd->bikgd", prob_round, value_blk, preferred_element_type=jnp.float32
    ).astype(jnp.bfloat16)
    attn_rows = attended.reshape(row_count, -1)
    attn_zx = by_zx(attn_rows, x_peers, z_peers)
    grad_out_part = jnp.einsum(
        "tzxi,tc->zxic", attn_zx, grad_out, preferred_element_type=jnp.float32
    ).astype(jnp.bfloat16)
    out_over_z = lax.psum_scatter(grad_out_part, "dz", scatter_dimension=0, tiled=True)[0]
    row_delta = jnp.sum(
        dattn_blk.astype(jnp.float32) * attended.astype(jnp.float32), axis=-1
    ).transpose(0, 2, 3, 1)
    grad_prob = jnp.einsum(
        "bikgd,bjkd->bkgij", dattn_blk, value_blk, preferred_element_type=jnp.float32
    )
    grad_scores = (prob_full * (grad_prob - row_delta[..., None]) * score_scale).astype(
        jnp.bfloat16
    )
    grad_queries = (
        jnp.einsum("bkgij,bjkd->bikgd", grad_scores, key_blk, preferred_element_type=jnp.float32)
        .astype(jnp.bfloat16)
        .reshape(row_count, -1)
    )
    grad_key_blk = jnp.einsum(
        "bkgij,bikgd->bjkd", grad_scores, query_blk, preferred_element_type=jnp.float32
    )
    grad_value_blk = jnp.einsum(
        "bkgij,bikgd->bjkd", prob_round, dattn_blk, preferred_element_type=jnp.float32
    )
    grad_key_ext = fold_blocks(grad_key_blk, window).reshape(row_count + window, -1)
    grad_value_ext = fold_blocks(grad_value_blk, window).reshape(row_count + window, -1)
    back_keys, back_values = (
        passed_along(grad_key_ext[:window].astype(jnp.bfloat16), DP_AXES, -1).astype(jnp.float32),
        passed_along(grad_value_ext[:window].astype(jnp.bfloat16), DP_AXES, -1).astype(jnp.float32),
    )
    own_keys = grad_key_ext[window:]
    own_values = grad_value_ext[window:]
    grad_keys = jnp.concatenate(
        [own_keys[:-window], own_keys[-window:] + back_keys], axis=0
    ).astype(jnp.bfloat16)
    grad_values = jnp.concatenate(
        [own_values[:-window], own_values[-window:] + back_values], axis=0
    ).astype(jnp.bfloat16)
    grad_qkv = jnp.concatenate([grad_queries, grad_keys, grad_values], axis=1)
    proj_by_mp = in_full.reshape((mp_peers, -1) + in_full.shape[1:])
    token_terms = jnp.einsum(
        "tc,mjrc->tmjr", grad_qkv, proj_by_mp, preferred_element_type=jnp.float32
    )
    grad_tokens = scatter_cols_mp(token_terms)
    tokens_zx = by_zx(tokens, x_peers, z_peers)
    grad_in_part = jnp.einsum(
        "tzxr,tc->zxrc", tokens_zx, grad_qkv, preferred_element_type=jnp.float32
    ).astype(jnp.bfloat16)
    in_over_z = lax.psum_scatter(grad_in_part, "dz", scatter_dimension=0, tiled=True)[0]
    out_over_z = out_over_z.reshape(x_peers, -1, in_width)
    both = jnp.concatenate([in_over_z, out_over_z], axis=1)
    over_x = lax.psum_scatter(both, "dx", scatter_dimension=0, tiled=True)[0].astype(jnp.float32)
    in_rows = w_query.shape[0]
    grad_in = over_x[:in_rows]
    grad_w_out = over_x[in_rows:].reshape(w_out.shape)
    grad_scale = 1.0 / math.sqrt(row_count * dp_peers)
    grad_in = grad_in * grad_scale
    return (
        grad_tokens,
        grad_in[:, :q_cols],
        grad_in[:, q_cols : q_cols + k_cols],
        grad_in[:, q_cols + k_cols :],
        grad_w_out * grad_scale,
    )


def split_mesh(mesh):
    dp = mesh.shape["dp"]
    try:
        x_peers = len({d.coords[0] for d in mesh.devices.flat})
    except AttributeError:
        x_peers = 4
    if dp % x_peers:
        x_peers = 1
    devices = mesh.devices.reshape(x_peers, dp // x_peers, mesh.shape["mp"])
    return Mesh(devices, ("dx", "dz", "mp"))


def solution(mesh):
    mesh = split_mesh(mesh)
    dp = DP_AXES
    return jax.shard_map(
        shards,
        mesh=mesh,
        in_specs=(
            P(dp, None),
            P(dp, "mp"),
            P(dp, "mp"),
            P(dp, "mp"),
            P(("mp",) + dp, None),
            P("mp"),
            P(dp, None),
        ),
        out_specs=(
            P(dp, "mp"),
            P(dp, "mp"),
            P(dp, "mp"),
            P(dp, "mp"),
            P(("mp",) + dp, None),
        ),
        check_vma=False,
    )
```

```python
import math

import jax
import jax.numpy as jnp
from jax import lax
from jax.sharding import Mesh, PartitionSpec as P

DH = 64
WINDOW = 128
LENGTH = 16384


masked_score = -1e30
DP_AXES = ("dx", "dz")
LANES = 128


def passed_along(array, axis, by):
    peers = lax.axis_size(axis)
    pairs = [(i, i + by) for i in range(peers) if 0 <= i + by < peers]
    return lax.ppermute(array, axis, pairs)


def contract_rows(left_side, right_side):
    return lax.dot_general(
        left_side, right_side, (((0,), (0,)), ((), ())), preferred_element_type=jnp.float32
    )


def contract_cols(left_side, right_side):
    return lax.dot_general(
        left_side, right_side, (((1,), (1,)), ((), ())), preferred_element_type=jnp.float32
    )


def band_mask(first_row, blocks, window):
    block_ids = jnp.arange(blocks, dtype=jnp.int32)[:, None, None] * window
    query_pos = first_row + block_ids + jnp.arange(window, dtype=jnp.int32)[None, :, None]
    key_pos = (
        first_row + block_ids + jnp.arange(2 * window, dtype=jnp.int32)[None, None, :] - window
    )
    offset = query_pos - key_pos
    same_resp = jnp.floor_divide(query_pos, LENGTH) == jnp.floor_divide(key_pos, LENGTH)
    return (offset >= 0) & (offset < window) & same_resp


def paired_blocks(extended, window):
    stacked = extended.reshape((-1, window) + extended.shape[1:])
    return jnp.concatenate([stacked[:-1], stacked[1:]], axis=1)


def fold_blocks(paired, window):
    widths = [(0, 0)] * (paired.ndim - 1)
    lower_half = jnp.pad(paired[:, :window], [(0, 1)] + widths)
    upper_half = jnp.pad(paired[:, window:], [(1, 0)] + widths)
    summed = lower_half + upper_half
    return summed.reshape((summed.shape[0] * window,) + summed.shape[2:])


def rows_of(array, lead):
    return array.reshape(array.shape[:1] + lead + (-1,))


def scatter_cols_mp(terms):
    peers = lax.axis_size("mp")
    me = lax.axis_index("mp")
    total = lax.dynamic_index_in_dim(terms, me, axis=1, keepdims=False)
    for shift in range(1, peers):
        dest = (me + shift) % peers
        piece = lax.dynamic_index_in_dim(terms, dest, axis=1, keepdims=False)
        pairs = [(i, (i + shift) % peers) for i in range(peers)]
        got = lax.ppermute(piece.astype(jnp.bfloat16), "mp", pairs)
        total = total + got.astype(jnp.float32)
    return total.reshape(total.shape[0], -1).astype(jnp.bfloat16)


def by_zx(rows, x_peers, z_peers):
    split = rows.reshape(rows.shape[0], x_peers, z_peers, -1)
    return split.transpose(0, 2, 1, 3)


def shards(tokens, w_query, w_key, w_value, w_out, sinks, grad_out):
    row_count = tokens.shape[0]
    window = WINDOW
    blocks = row_count // window
    score_scale = 1.0 / math.sqrt(DH)
    x_peers = lax.axis_size("dx")
    z_peers = lax.axis_size("dz")
    mp_peers = lax.axis_size("mp")
    dp_peers = x_peers * z_peers
    q_cols, k_cols, v_cols = w_query.shape[1], w_key.shape[1], w_value.shape[1]
    in_width = q_cols + k_cols + v_cols
    out_rows = w_out.shape[0]
    packed = jnp.concatenate(
        [w_query, w_key, w_value, w_out.reshape(w_query.shape[0], -1)], axis=1
    )
    gathered = lax.all_gather(packed, DP_AXES, axis=0, tiled=False)
    in_full = gathered[:, :, :in_width]
    out_packed = gathered[:, :, in_width:]
    kv_heads = k_cols // DH
    group_size = q_cols // DH // kv_heads
    tokens_blk = rows_of(tokens, (dp_peers,))
    qkv = jnp.einsum("tdr,drc->tc", tokens_blk, in_full, preferred_element_type=jnp.float32).astype(
        jnp.bfloat16
    )
    queries = qkv[:, :q_cols]
    key_rows = qkv[:, q_cols : q_cols + k_cols]
    value_rows = qkv[:, q_cols + k_cols :]
    rim_keys, rim_values = passed_along((key_rows[-window:], value_rows[-window:]), DP_AXES, 1)
    first_row = (lax.axis_index("dx") * z_peers + lax.axis_index("dz")) * row_count
    ext_keys = jnp.concatenate([rim_keys, key_rows], axis=0).reshape(
        row_count + window, kv_heads, DH
    )
    ext_values = jnp.concatenate([rim_values, value_rows], axis=0).reshape(
        row_count + window, kv_heads, DH
    )
    key_blk = paired_blocks(ext_keys, window)
    value_blk = paired_blocks(ext_values, window)
    query_blk = queries.reshape(blocks, window, kv_heads, group_size, DH)
    scores = (
        jnp.einsum("bikgd,bjkd->bkgij", query_blk, key_blk, preferred_element_type=jnp.float32)
        * score_scale
    )
    allowed = band_mask(first_row, blocks, window)[:, None, None]
    scores = jnp.where(allowed, scores, masked_score)
    sink_row = sinks.reshape(kv_heads, group_size)[None, :, :, None]
    row_peak = jnp.maximum(jnp.max(scores, axis=-1), sink_row)
    row_total = jnp.exp(sink_row - row_peak) + jnp.sum(
        jnp.exp(scores - row_peak[..., None]), axis=-1
    )
    log_total = row_peak + jnp.log(row_total)
    prob_full = jnp.exp(scores - log_total[..., None])
    prob_round = prob_full.astype(jnp.bfloat16)
    attended = jnp.einsum(
        "bkgij,bjkd->bikgd", prob_round, value_blk, preferred_element_type=jnp.float32
    ).astype(jnp.bfloat16)
    attn_rows = attended.reshape(row_count, -1)
    attn_zx = by_zx(attn_rows, x_peers, z_peers)
    grad_out_part = jnp.einsum(
        "tzxi,tc->zxic", attn_zx, grad_out, preferred_element_type=jnp.float32
    ).astype(jnp.bfloat16)
    out_packed, grad_out_part = lax.optimization_barrier((out_packed, grad_out_part))
    out_over_z = lax.psum_scatter(grad_out_part, "dz", scatter_dimension=0, tiled=True)[0]
    full_out = out_packed.reshape((-1,) + w_out.shape[1:])
    grad_attn = contract_cols(grad_out, full_out).astype(jnp.bfloat16)
    dattn_blk = grad_attn.reshape(blocks, window, kv_heads, group_size, DH)
    row_delta = jnp.sum(
        dattn_blk.astype(jnp.float32) * attended.astype(jnp.float32), axis=-1
    ).transpose(0, 2, 3, 1)
    grad_prob = jnp.einsum(
        "bikgd,bjkd->bkgij", dattn_blk, value_blk, preferred_element_type=jnp.float32
    )
    grad_scores = (prob_full * (grad_prob - row_delta[..., None]) * score_scale).astype(
        jnp.bfloat16
    )
    grad_queries = (
        jnp.einsum("bkgij,bjkd->bikgd", grad_scores, key_blk, preferred_element_type=jnp.float32)
        .astype(jnp.bfloat16)
        .reshape(row_count, -1)
    )
    grad_key_blk = jnp.einsum(
        "bkgij,bikgd->bjkd", grad_scores, query_blk, preferred_element_type=jnp.float32
    )
    grad_value_blk = jnp.einsum(
        "bkgij,bikgd->bjkd", prob_round, dattn_blk, preferred_element_type=jnp.float32
    )
    grad_key_ext = fold_blocks(grad_key_blk, window).reshape(row_count + window, -1)
    grad_value_ext = fold_blocks(grad_value_blk, window).reshape(row_count + window, -1)
    back_keys, back_values = (
        passed_along(grad_key_ext[:window].astype(jnp.bfloat16), DP_AXES, -1).astype(jnp.float32),
        passed_along(grad_value_ext[:window].astype(jnp.bfloat16), DP_AXES, -1).astype(jnp.float32),
    )
    own_keys = grad_key_ext[window:]
    own_values = grad_value_ext[window:]
    grad_keys = jnp.concatenate(
        [own_keys[:-window], own_keys[-window:] + back_keys], axis=0
    ).astype(jnp.bfloat16)
    grad_values = jnp.concatenate(
        [own_values[:-window], own_values[-window:] + back_values], axis=0
    ).astype(jnp.bfloat16)
    grad_qkv = jnp.concatenate([grad_queries, grad_keys, grad_values], axis=1)
    proj_by_mp = in_full.reshape((mp_peers, -1) + in_full.shape[1:])
    token_terms = jnp.einsum(
        "tc,mjrc->tmjr", grad_qkv, proj_by_mp, preferred_element_type=jnp.float32
    )
    grad_tokens = scatter_cols_mp(token_terms)
    tokens_zx = by_zx(tokens, x_peers, z_peers)
    grad_in_part = jnp.einsum(
        "tzxr,tc->zxrc", tokens_zx, grad_qkv, preferred_element_type=jnp.float32
    ).astype(jnp.bfloat16)
    grad_tokens, grad_in_part = lax.optimization_barrier((grad_tokens, grad_in_part))
    in_over_z = lax.psum_scatter(grad_in_part, "dz", scatter_dimension=0, tiled=True)[0]
    out_over_z = out_over_z.reshape(x_peers, -1, in_width)
    both = jnp.concatenate([in_over_z, out_over_z], axis=1)
    over_x = lax.psum_scatter(both, "dx", scatter_dimension=0, tiled=True)[0].astype(jnp.float32)
    in_rows = w_query.shape[0]
    grad_in = over_x[:in_rows]
    grad_w_out = over_x[in_rows:].reshape(w_out.shape)
    grad_scale = 1.0 / math.sqrt(row_count * dp_peers)
    grad_in = grad_in * grad_scale
    return (
        grad_tokens,
        grad_in[:, :q_cols],
        grad_in[:, q_cols : q_cols + k_cols],
        grad_in[:, q_cols + k_cols :],
        grad_w_out * grad_scale,
    )


def split_mesh(mesh):
    dp = mesh.shape["dp"]
    try:
        x_peers = len({d.coords[0] for d in mesh.devices.flat})
    except AttributeError:
        x_peers = 4
    if dp % x_peers:
        x_peers = 1
    devices = mesh.devices.reshape(x_peers, dp // x_peers, mesh.shape["mp"])
    return Mesh(devices, ("dx", "dz", "mp"))


def solution(mesh):
    mesh = split_mesh(mesh)
    dp = DP_AXES
    return jax.shard_map(
        shards,
        mesh=mesh,
        in_specs=(
            P(dp, None),
            P(dp, "mp"),
            P(dp, "mp"),
            P(dp, "mp"),
            P(("mp",) + dp, None),
            P("mp"),
            P(dp, None),
        ),
        out_specs=(
            P(dp, "mp"),
            P(dp, "mp"),
            P(dp, "mp"),
            P(dp, "mp"),
            P(("mp",) + dp, None),
        ),
        check_vma=False,
    )
```

```python
import math

import jax
import jax.numpy as jnp
from jax import lax
from jax.sharding import Mesh, PartitionSpec as P

DH = 64
WINDOW = 128
LENGTH = 16384


masked_score = -1e30
DP_AXES = ("dx", "dz")
LANES = 128
CORES = 2


def passed_along(array, axis, by):
    peers = lax.axis_size(axis)
    pairs = [(i, i + by) for i in range(peers) if 0 <= i + by < peers]
    return lax.ppermute(array, axis, pairs)


def contract_rows(left_side, right_side):
    return lax.dot_general(
        left_side, right_side, (((0,), (0,)), ((), ())), preferred_element_type=jnp.float32
    )


def contract_cols(left_side, right_side):
    return lax.dot_general(
        left_side, right_side, (((1,), (1,)), ((), ())), preferred_element_type=jnp.float32
    )


def band_mask(first_row, blocks, window):
    block_ids = jnp.arange(blocks, dtype=jnp.int32)[:, None, None] * window
    query_pos = first_row + block_ids + jnp.arange(window, dtype=jnp.int32)[None, :, None]
    key_pos = (
        first_row + block_ids + jnp.arange(2 * window, dtype=jnp.int32)[None, None, :] - window
    )
    offset = query_pos - key_pos
    same_resp = jnp.floor_divide(query_pos, LENGTH) == jnp.floor_divide(key_pos, LENGTH)
    return (offset >= 0) & (offset < window) & same_resp


def paired_blocks(extended, window):
    stacked = extended.reshape((-1, window) + extended.shape[1:])
    return jnp.concatenate([stacked[:-1], stacked[1:]], axis=1)


def fold_blocks(paired, window):
    widths = [(0, 0)] * (paired.ndim - 1)
    lower_half = jnp.pad(paired[:, :window], [(0, 1)] + widths)
    upper_half = jnp.pad(paired[:, window:], [(1, 0)] + widths)
    summed = lower_half + upper_half
    return summed.reshape((summed.shape[0] * window,) + summed.shape[2:])


def rows_of(array, lead):
    return array.reshape(array.shape[:1] + lead + (-1,))


def scatter_cols_mp(terms, cores):
    peers = lax.axis_size("mp")
    chips = peers // cores
    me = lax.axis_index("mp")
    my_chip, my_core = me // cores, me % cores
    by_core = terms.reshape((terms.shape[0], chips, cores) + terms.shape[2:])
    total = lax.dynamic_index_in_dim(by_core, my_core, axis=2, keepdims=False).astype(jnp.float32)
    for shift in range(1, cores):
        dest = (my_core + shift) % cores
        piece = lax.dynamic_index_in_dim(by_core, dest, axis=2, keepdims=False)
        pairs = [(k, k - k % cores + (k % cores + shift) % cores) for k in range(peers)]
        got = lax.ppermute(piece.astype(jnp.bfloat16), "mp", pairs)
        total = total + got.astype(jnp.float32)
    result = lax.dynamic_index_in_dim(total, my_chip, axis=1, keepdims=False)
    for shift in range(1, chips):
        dest = (my_chip + shift) % chips
        piece = lax.dynamic_index_in_dim(total, dest, axis=1, keepdims=False)
        pairs = [(k, ((k // cores + shift) % chips) * cores + k % cores) for k in range(peers)]
        got = lax.ppermute(piece.astype(jnp.bfloat16), "mp", pairs)
        result = result + got.astype(jnp.float32)
    return result.reshape(result.shape[0], -1).astype(jnp.bfloat16)


def by_zx(rows, x_peers, z_peers):
    split = rows.reshape(rows.shape[0], x_peers, z_peers, -1)
    return split.transpose(0, 2, 1, 3)


def shards(tokens, w_query, w_key, w_value, w_out, sinks, grad_out):
    row_count = tokens.shape[0]
    window = WINDOW
    blocks = row_count // window
    score_scale = 1.0 / math.sqrt(DH)
    x_peers = lax.axis_size("dx")
    z_peers = lax.axis_size("dz")
    mp_peers = lax.axis_size("mp")
    dp_peers = x_peers * z_peers
    q_cols, k_cols, v_cols = w_query.shape[1], w_key.shape[1], w_value.shape[1]
    in_width = q_cols + k_cols + v_cols
    out_rows = w_out.shape[0]
    packed = jnp.concatenate(
        [w_query, w_key, w_value, w_out.reshape(w_query.shape[0], -1)], axis=1
    )
    gathered = lax.all_gather(packed, DP_AXES, axis=0, tiled=False)
    in_full = gathered[:, :, :in_width]
    kv_heads = k_cols // DH
    group_size = q_cols // DH // kv_heads
    tokens_blk = rows_of(tokens, (dp_peers,))
    qkv = jnp.einsum("tdr,drc->tc", tokens_blk, in_full, preferred_element_type=jnp.float32).astype(
        jnp.bfloat16
    )
    queries = qkv[:, :q_cols]
    key_rows = qkv[:, q_cols : q_cols + k_cols]
    value_rows = qkv[:, q_cols + k_cols :]
    rim_keys, rim_values = passed_along((key_rows[-window:], value_rows[-window:]), DP_AXES, 1)
    first_row = (lax.axis_index("dx") * z_peers + lax.axis_index("dz")) * row_count
    ext_keys = jnp.concatenate([rim_keys, key_rows], axis=0).reshape(
        row_count + window, kv_heads, DH
    )
    ext_values = jnp.concatenate([rim_values, value_rows], axis=0).reshape(
        row_count + window, kv_heads, DH
    )
    key_blk = paired_blocks(ext_keys, window)
    value_blk = paired_blocks(ext_values, window)
    query_blk = queries.reshape(blocks, window, kv_heads, group_size, DH)
    scores = (
        jnp.einsum("bikgd,bjkd->bkgij", query_blk, key_blk, preferred_element_type=jnp.float32)
        * score_scale
    )
    allowed = band_mask(first_row, blocks, window)[:, None, None]
    scores = jnp.where(allowed, scores, masked_score)
    sink_row = sinks.reshape(kv_heads, group_size)[None, :, :, None]
    row_peak = jnp.maximum(jnp.max(scores, axis=-1), sink_row)
    row_total = jnp.exp(sink_row - row_peak) + jnp.sum(
        jnp.exp(scores - row_peak[..., None]), axis=-1
    )
    log_total = row_peak + jnp.log(row_total)
    prob_full = jnp.exp(scores - log_total[..., None])
    prob_round = prob_full.astype(jnp.bfloat16)
    attended = jnp.einsum(
        "bkgij,bjkd->bikgd", prob_round, value_blk, preferred_element_type=jnp.float32
    ).astype(jnp.bfloat16)
    attn_rows = attended.reshape(row_count, -1)
    attn_zx = by_zx(attn_rows, x_peers, z_peers)
    grad_out_part = jnp.einsum(
        "tzxi,tc->zxic", attn_zx, grad_out, preferred_element_type=jnp.float32
    ).astype(jnp.bfloat16)
    late_gathered, grad_out_part = lax.optimization_barrier((gathered, grad_out_part))
    out_over_z = lax.psum_scatter(grad_out_part, "dz", scatter_dimension=0, tiled=True)[0]
    full_out = late_gathered[:, :, in_width:].reshape((-1,) + w_out.shape[1:])
    grad_attn = contract_cols(grad_out, full_out).astype(jnp.bfloat16)
    dattn_blk = grad_attn.reshape(blocks, window, kv_heads, group_size, DH)
    row_delta = jnp.sum(
        dattn_blk.astype(jnp.float32) * attended.astype(jnp.float32), axis=-1
    ).transpose(0, 2, 3, 1)
    grad_prob = jnp.einsum(
        "bikgd,bjkd->bkgij", dattn_blk, value_blk, preferred_element_type=jnp.float32
    )
    grad_scores = (prob_full * (grad_prob - row_delta[..., None]) * score_scale).astype(
        jnp.bfloat16
    )
    grad_queries = (
        jnp.einsum("bkgij,bjkd->bikgd", grad_scores, key_blk, preferred_element_type=jnp.float32)
        .astype(jnp.bfloat16)
        .reshape(row_count, -1)
    )
    grad_key_blk = jnp.einsum(
        "bkgij,bikgd->bjkd", grad_scores, query_blk, preferred_element_type=jnp.float32
    )
    grad_value_blk = jnp.einsum(
        "bkgij,bikgd->bjkd", prob_round, dattn_blk, preferred_element_type=jnp.float32
    )
    grad_key_ext = fold_blocks(grad_key_blk, window).reshape(row_count + window, -1)
    grad_value_ext = fold_blocks(grad_value_blk, window).reshape(row_count + window, -1)
    back_keys, back_values = (
        passed_along(grad_key_ext[:window].astype(jnp.bfloat16), DP_AXES, -1).astype(jnp.float32),
        passed_along(grad_value_ext[:window].astype(jnp.bfloat16), DP_AXES, -1).astype(jnp.float32),
    )
    own_keys = grad_key_ext[window:]
    own_values = grad_value_ext[window:]
    grad_keys = jnp.concatenate(
        [own_keys[:-window], own_keys[-window:] + back_keys], axis=0
    ).astype(jnp.bfloat16)
    grad_values = jnp.concatenate(
        [own_values[:-window], own_values[-window:] + back_values], axis=0
    ).astype(jnp.bfloat16)
    grad_qkv = jnp.concatenate([grad_queries, grad_keys, grad_values], axis=1)
    grad_wide = jnp.pad(grad_qkv, ((0, 0), (0, gathered.shape[2] - in_width)))
    proj_by_mp = late_gathered.reshape((mp_peers, -1) + gathered.shape[1:])
    token_terms = jnp.einsum(
        "tc,mjrc->tmjr", grad_wide, proj_by_mp, preferred_element_type=jnp.float32
    )
    grad_tokens = scatter_cols_mp(token_terms, CORES)
    tokens_zx = by_zx(tokens, x_peers, z_peers)
    grad_in_part = jnp.einsum(
        "tzxr,tc->zxrc", tokens_zx, grad_qkv, preferred_element_type=jnp.float32
    ).astype(jnp.bfloat16)
    grad_tokens, grad_in_part = lax.optimization_barrier((grad_tokens, grad_in_part))
    in_over_z = lax.psum_scatter(grad_in_part, "dz", scatter_dimension=0, tiled=True)[0]
    out_over_z = out_over_z.reshape(x_peers, -1, in_width)
    both = jnp.concatenate([in_over_z, out_over_z], axis=1)
    over_x = lax.psum_scatter(both, "dx", scatter_dimension=0, tiled=True)[0].astype(jnp.float32)
    in_rows = w_query.shape[0]
    grad_in = over_x[:in_rows]
    grad_w_out = over_x[in_rows:].reshape(w_out.shape)
    grad_scale = 1.0 / math.sqrt(row_count * dp_peers)
    grad_in = grad_in * grad_scale
    return (
        grad_tokens,
        grad_in[:, :q_cols],
        grad_in[:, q_cols : q_cols + k_cols],
        grad_in[:, q_cols + k_cols :],
        grad_w_out * grad_scale,
    )


def split_mesh(mesh):
    dp = mesh.shape["dp"]
    try:
        x_peers = len({d.coords[0] for d in mesh.devices.flat})
    except AttributeError:
        x_peers = 4
    if dp % x_peers:
        x_peers = 1
    devices = mesh.devices.reshape(x_peers, dp // x_peers, mesh.shape["mp"])
    return Mesh(devices, ("dx", "dz", "mp"))


def solution(mesh):
    mesh = split_mesh(mesh)
    dp = DP_AXES
    return jax.shard_map(
        shards,
        mesh=mesh,
        in_specs=(
            P(dp, None),
            P(dp, "mp"),
            P(dp, "mp"),
            P(dp, "mp"),
            P(("mp",) + dp, None),
            P("mp"),
            P(dp, None),
        ),
        out_specs=(
            P(dp, "mp"),
            P(dp, "mp"),
            P(dp, "mp"),
            P(dp, "mp"),
            P(("mp",) + dp, None),
        ),
        check_vma=False,
    )
```

```python
import math

import jax
import jax.numpy as jnp
from jax import lax
from jax.sharding import Mesh, PartitionSpec as P

DH = 64
WINDOW = 128
LENGTH = 16384


masked_score = -1e30
DP_AXES = ("dx", "dz")
LANES = 128
CORES = 2


def passed_along(array, axis, by):
    peers = lax.axis_size(axis)
    pairs = [(i, i + by) for i in range(peers) if 0 <= i + by < peers]
    return lax.ppermute(array, axis, pairs)


def contract_rows(left_side, right_side):
    return lax.dot_general(
        left_side, right_side, (((0,), (0,)), ((), ())), preferred_element_type=jnp.float32
    )


def contract_cols(left_side, right_side):
    return lax.dot_general(
        left_side, right_side, (((1,), (1,)), ((), ())), preferred_element_type=jnp.float32
    )


def band_mask(first_row, blocks, window):
    block_ids = jnp.arange(blocks, dtype=jnp.int32)[:, None, None] * window
    query_pos = first_row + block_ids + jnp.arange(window, dtype=jnp.int32)[None, :, None]
    key_pos = (
        first_row + block_ids + jnp.arange(2 * window, dtype=jnp.int32)[None, None, :] - window
    )
    offset = query_pos - key_pos
    same_resp = jnp.floor_divide(query_pos, LENGTH) == jnp.floor_divide(key_pos, LENGTH)
    return (offset >= 0) & (offset < window) & same_resp


def paired_blocks(extended, window):
    stacked = extended.reshape((-1, window) + extended.shape[1:])
    return jnp.concatenate([stacked[:-1], stacked[1:]], axis=1)


def fold_blocks(paired, window):
    widths = [(0, 0)] * (paired.ndim - 1)
    lower_half = jnp.pad(paired[:, :window], [(0, 1)] + widths)
    upper_half = jnp.pad(paired[:, window:], [(1, 0)] + widths)
    summed = lower_half + upper_half
    return summed.reshape((summed.shape[0] * window,) + summed.shape[2:])


def rows_of(array, lead):
    return array.reshape(array.shape[:1] + lead + (-1,))


def scatter_cols_mp(terms, cores):
    peers = lax.axis_size("mp")
    chips = peers // cores
    me = lax.axis_index("mp")
    my_chip, my_core = me // cores, me % cores
    by_core = terms.reshape((terms.shape[0], chips, cores) + terms.shape[2:])
    total = lax.dynamic_index_in_dim(by_core, my_core, axis=2, keepdims=False).astype(jnp.float32)
    for shift in range(1, cores):
        dest = (my_core + shift) % cores
        piece = lax.dynamic_index_in_dim(by_core, dest, axis=2, keepdims=False)
        pairs = [(k, k - k % cores + (k % cores + shift) % cores) for k in range(peers)]
        got = lax.ppermute(piece.astype(jnp.bfloat16), "mp", pairs)
        total = total + got.astype(jnp.float32)
    result = lax.dynamic_index_in_dim(total, my_chip, axis=1, keepdims=False)
    for shift in range(1, chips):
        dest = (my_chip + shift) % chips
        piece = lax.dynamic_index_in_dim(total, dest, axis=1, keepdims=False)
        pairs = [(k, ((k // cores + shift) % chips) * cores + k % cores) for k in range(peers)]
        got = lax.ppermute(piece.astype(jnp.bfloat16), "mp", pairs)
        result = result + got.astype(jnp.float32)
    return result.reshape(result.shape[0], -1).astype(jnp.bfloat16)


def scatter_rows_x(parts):
    peers = lax.axis_size("dx")
    me = lax.axis_index("dx")
    total = lax.dynamic_index_in_dim(parts, me, axis=0, keepdims=False).astype(jnp.float32)
    for shift in range(1, peers):
        dest = (me + shift) % peers
        piece = lax.dynamic_index_in_dim(parts, dest, axis=0, keepdims=False)
        pairs = [(i, (i + shift) % peers) for i in range(peers)]
        total = total + lax.ppermute(piece, "dx", pairs).astype(jnp.float32)
    return total


def by_zx(rows, x_peers, z_peers):
    split = rows.reshape(rows.shape[0], x_peers, z_peers, -1)
    return split.transpose(0, 2, 1, 3)


def shards(tokens, w_query, w_key, w_value, w_out, sinks, grad_out):
    row_count = tokens.shape[0]
    window = WINDOW
    blocks = row_count // window
    score_scale = 1.0 / math.sqrt(DH)
    x_peers = lax.axis_size("dx")
    z_peers = lax.axis_size("dz")
    mp_peers = lax.axis_size("mp")
    dp_peers = x_peers * z_peers
    q_cols, k_cols, v_cols = w_query.shape[1], w_key.shape[1], w_value.shape[1]
    in_width = q_cols + k_cols + v_cols
    out_rows = w_out.shape[0]
    packed = jnp.concatenate(
        [w_query, w_key, w_value, w_out.reshape(w_query.shape[0], -1)], axis=1
    )
    gathered = lax.all_gather(packed, DP_AXES, axis=0, tiled=False)
    in_full = gathered[:, :, :in_width]
    kv_heads = k_cols // DH
    group_size = q_cols // DH // kv_heads
    tokens_blk = rows_of(tokens, (dp_peers,))
    qkv = jnp.einsum("tdr,drc->tc", tokens_blk, in_full, preferred_element_type=jnp.float32).astype(
        jnp.bfloat16
    )
    queries = qkv[:, :q_cols]
    key_rows = qkv[:, q_cols : q_cols + k_cols]
    value_rows = qkv[:, q_cols + k_cols :]
    rim = passed_along(qkv[-window:, q_cols:], DP_AXES, 1)
    rim_keys, rim_values = rim[:, :k_cols], rim[:, k_cols:]
    first_row = (lax.axis_index("dx") * z_peers + lax.axis_index("dz")) * row_count
    ext_keys = jnp.concatenate([rim_keys, key_rows], axis=0).reshape(
        row_count + window, kv_heads, DH
    )
    ext_values = jnp.concatenate([rim_values, value_rows], axis=0).reshape(
        row_count + window, kv_heads, DH
    )
    key_blk = paired_blocks(ext_keys, window)
    value_blk = paired_blocks(ext_values, window)
    query_blk = queries.reshape(blocks, window, kv_heads, group_size, DH)
    scores = (
        jnp.einsum("bikgd,bjkd->bkgij", query_blk, key_blk, preferred_element_type=jnp.float32)
        * score_scale
    )
    allowed = band_mask(first_row, blocks, window)[:, None, None]
    scores = jnp.where(allowed, scores, masked_score)
    sink_row = sinks.reshape(kv_heads, group_size)[None, :, :, None]
    row_peak = jnp.maximum(jnp.max(scores, axis=-1), sink_row)
    row_total = jnp.exp(sink_row - row_peak) + jnp.sum(
        jnp.exp(scores - row_peak[..., None]), axis=-1
    )
    log_total = row_peak + jnp.log(row_total)
    prob_full = jnp.exp(scores - log_total[..., None])
    prob_round = prob_full.astype(jnp.bfloat16)
    attended = jnp.einsum(
        "bkgij,bjkd->bikgd", prob_round, value_blk, preferred_element_type=jnp.float32
    ).astype(jnp.bfloat16)
    attn_rows = attended.reshape(row_count, -1)
    attn_zx = by_zx(attn_rows, x_peers, z_peers)
    grad_out_part = jnp.einsum(
        "tzxi,tc->zxic", attn_zx, grad_out, preferred_element_type=jnp.float32
    ).astype(jnp.bfloat16)
    late_gathered, grad_out_part = lax.optimization_barrier((gathered, grad_out_part))
    out_over_z = lax.psum_scatter(grad_out_part, "dz", scatter_dimension=0, tiled=True)[0]
    full_out = late_gathered[:, :, in_width:].reshape((-1,) + w_out.shape[1:])
    grad_attn = contract_cols(grad_out, full_out).astype(jnp.bfloat16)
    dattn_blk = grad_attn.reshape(blocks, window, kv_heads, group_size, DH)
    row_delta = jnp.sum(
        dattn_blk.astype(jnp.float32) * attended.astype(jnp.float32), axis=-1
    ).transpose(0, 2, 3, 1)
    grad_prob = jnp.einsum(
        "bikgd,bjkd->bkgij", dattn_blk, value_blk, preferred_element_type=jnp.float32
    )
    grad_scores = (prob_full * (grad_prob - row_delta[..., None]) * score_scale).astype(
        jnp.bfloat16
    )
    grad_queries = (
        jnp.einsum("bkgij,bjkd->bikgd", grad_scores, key_blk, preferred_element_type=jnp.float32)
        .astype(jnp.bfloat16)
        .reshape(row_count, -1)
    )
    grad_key_blk = jnp.einsum(
        "bkgij,bikgd->bjkd", grad_scores, query_blk, preferred_element_type=jnp.float32
    )
    grad_value_blk = jnp.einsum(
        "bkgij,bikgd->bjkd", prob_round, dattn_blk, preferred_element_type=jnp.float32
    )
    grad_key_ext = fold_blocks(grad_key_blk, window).reshape(row_count + window, -1)
    grad_value_ext = fold_blocks(grad_value_blk, window).reshape(row_count + window, -1)
    back_rim = jnp.concatenate([grad_key_ext[:window], grad_value_ext[:window]], axis=1)
    back_rim = passed_along(back_rim.astype(jnp.bfloat16), DP_AXES, -1).astype(jnp.float32)
    back_keys, back_values = back_rim[:, :k_cols], back_rim[:, k_cols:]
    own_keys = grad_key_ext[window:]
    own_values = grad_value_ext[window:]
    grad_keys = jnp.concatenate(
        [own_keys[:-window], own_keys[-window:] + back_keys], axis=0
    ).astype(jnp.bfloat16)
    grad_values = jnp.concatenate(
        [own_values[:-window], own_values[-window:] + back_values], axis=0
    ).astype(jnp.bfloat16)
    grad_qkv = jnp.concatenate([grad_queries, grad_keys, grad_values], axis=1)
    grad_wide = jnp.pad(grad_qkv, ((0, 0), (0, gathered.shape[2] - in_width)))
    proj_by_mp = late_gathered.reshape((mp_peers, -1) + gathered.shape[1:])
    token_terms = jnp.einsum(
        "tc,mjrc->tmjr", grad_wide, proj_by_mp, preferred_element_type=jnp.float32
    )
    grad_tokens = scatter_cols_mp(token_terms, CORES)
    tokens_zx = by_zx(tokens, x_peers, z_peers)
    grad_in_part = jnp.einsum(
        "tzxr,tc->zxrc", tokens_zx, grad_qkv, preferred_element_type=jnp.float32
    ).astype(jnp.bfloat16)
    grad_tokens, grad_in_part = lax.optimization_barrier((grad_tokens, grad_in_part))
    in_over_z = lax.psum_scatter(grad_in_part, "dz", scatter_dimension=0, tiled=True)[0]
    out_over_z = out_over_z.reshape(x_peers, -1, in_width)
    both = jnp.concatenate([in_over_z, out_over_z], axis=1)
    over_x = scatter_rows_x(both)
    in_rows = w_query.shape[0]
    grad_in = over_x[:in_rows]
    grad_w_out = over_x[in_rows:].reshape(w_out.shape)
    grad_scale = 1.0 / math.sqrt(row_count * dp_peers)
    grad_in = grad_in * grad_scale
    return (
        grad_tokens,
        grad_in[:, :q_cols],
        grad_in[:, q_cols : q_cols + k_cols],
        grad_in[:, q_cols + k_cols :],
        grad_w_out * grad_scale,
    )


def split_mesh(mesh):
    dp = mesh.shape["dp"]
    try:
        x_peers = len({d.coords[0] for d in mesh.devices.flat})
    except AttributeError:
        x_peers = 4
    if dp % x_peers:
        x_peers = 1
    devices = mesh.devices.reshape(x_peers, dp // x_peers, mesh.shape["mp"])
    return Mesh(devices, ("dx", "dz", "mp"))


def solution(mesh):
    mesh = split_mesh(mesh)
    dp = DP_AXES
    return jax.shard_map(
        shards,
        mesh=mesh,
        in_specs=(
            P(dp, None),
            P(dp, "mp"),
            P(dp, "mp"),
            P(dp, "mp"),
            P(("mp",) + dp, None),
            P("mp"),
            P(dp, None),
        ),
        out_specs=(
            P(dp, "mp"),
            P(dp, "mp"),
            P(dp, "mp"),
            P(dp, "mp"),
            P(("mp",) + dp, None),
        ),
        check_vma=False,
    )
```

```python
import math

import jax
import jax.numpy as jnp
from jax import lax
from jax.sharding import Mesh, PartitionSpec as P

DH = 64
WINDOW = 128
LENGTH = 16384


masked_score = -1e30
DP_AXES = ("dx", "dz")
LANES = 128
CORES = 2


def passed_along(array, axis, by):
    peers = lax.axis_size(axis)
    pairs = [(i, i + by) for i in range(peers) if 0 <= i + by < peers]
    return lax.ppermute(array, axis, pairs)


def contract_rows(left_side, right_side):
    return lax.dot_general(
        left_side, right_side, (((0,), (0,)), ((), ())), preferred_element_type=jnp.float32
    )


def contract_cols(left_side, right_side):
    return lax.dot_general(
        left_side, right_side, (((1,), (1,)), ((), ())), preferred_element_type=jnp.float32
    )


def band_mask(first_row, blocks, window):
    block_ids = jnp.arange(blocks, dtype=jnp.int32)[:, None, None] * window
    query_pos = first_row + block_ids + jnp.arange(window, dtype=jnp.int32)[None, :, None]
    key_pos = (
        first_row + block_ids + jnp.arange(2 * window, dtype=jnp.int32)[None, None, :] - window
    )
    offset = query_pos - key_pos
    same_resp = jnp.floor_divide(query_pos, LENGTH) == jnp.floor_divide(key_pos, LENGTH)
    return (offset >= 0) & (offset < window) & same_resp


def paired_blocks(extended, window):
    stacked = extended.reshape((-1, window) + extended.shape[1:])
    return jnp.concatenate([stacked[:-1], stacked[1:]], axis=1)


def fold_blocks(paired, window):
    widths = [(0, 0)] * (paired.ndim - 1)
    lower_half = jnp.pad(paired[:, :window], [(0, 1)] + widths)
    upper_half = jnp.pad(paired[:, window:], [(1, 0)] + widths)
    summed = lower_half + upper_half
    return summed.reshape((summed.shape[0] * window,) + summed.shape[2:])


def rows_of(array, lead):
    return array.reshape(array.shape[:1] + lead + (-1,))


def scatter_cols_mp(terms, cores):
    peers = lax.axis_size("mp")
    chips = peers // cores
    me = lax.axis_index("mp")
    my_chip, my_core = me // cores, me % cores
    by_core = terms.reshape((terms.shape[0], chips, cores) + terms.shape[2:])
    total = lax.dynamic_index_in_dim(by_core, my_core, axis=2, keepdims=False).astype(jnp.float32)
    for shift in range(1, cores):
        dest = (my_core + shift) % cores
        piece = lax.dynamic_index_in_dim(by_core, dest, axis=2, keepdims=False)
        pairs = [(k, k - k % cores + (k % cores + shift) % cores) for k in range(peers)]
        got = lax.ppermute(piece.astype(jnp.bfloat16), "mp", pairs)
        total = total + got.astype(jnp.float32)
    result = lax.dynamic_index_in_dim(total, my_chip, axis=1, keepdims=False)
    for shift in range(1, chips):
        dest = (my_chip + shift) % chips
        piece = lax.dynamic_index_in_dim(total, dest, axis=1, keepdims=False)
        pairs = [(k, ((k // cores + shift) % chips) * cores + k % cores) for k in range(peers)]
        got = lax.ppermute(piece.astype(jnp.bfloat16), "mp", pairs)
        result = result + got.astype(jnp.float32)
    return result.reshape(result.shape[0], -1).astype(jnp.bfloat16)


def scatter_rows_x(parts):
    peers = lax.axis_size("dx")
    me = lax.axis_index("dx")
    total = lax.dynamic_index_in_dim(parts, me, axis=0, keepdims=False).astype(jnp.float32)
    for shift in range(1, peers):
        dest = (me + shift) % peers
        piece = lax.dynamic_index_in_dim(parts, dest, axis=0, keepdims=False)
        pairs = [(i, (i + shift) % peers) for i in range(peers)]
        total = total + lax.ppermute(piece, "dx", pairs).astype(jnp.float32)
    return total


def by_zx(rows, x_peers, z_peers):
    split = rows.reshape(rows.shape[0], x_peers, z_peers, -1)
    return split.transpose(0, 2, 1, 3)


def shards(tokens, w_query, w_key, w_value, w_out, sinks, grad_out):
    row_count = tokens.shape[0]
    window = WINDOW
    blocks = row_count // window
    score_scale = 1.0 / math.sqrt(DH)
    x_peers = lax.axis_size("dx")
    z_peers = lax.axis_size("dz")
    mp_peers = lax.axis_size("mp")
    dp_peers = x_peers * z_peers
    q_cols, k_cols, v_cols = w_query.shape[1], w_key.shape[1], w_value.shape[1]
    in_width = q_cols + k_cols + v_cols
    out_rows = w_out.shape[0]
    packed = jnp.concatenate(
        [w_query, w_key, w_value, w_out.reshape(w_query.shape[0], -1)], axis=1
    )
    gathered = lax.all_gather(packed, DP_AXES, axis=0, tiled=False)
    in_full = gathered[:, :, :in_width]
    kv_heads = k_cols // DH
    group_size = q_cols // DH // kv_heads
    tokens_blk = rows_of(tokens, (dp_peers,))
    qkv = jnp.einsum("tdr,drc->tc", tokens_blk, in_full, preferred_element_type=jnp.float32).astype(
        jnp.bfloat16
    )
    queries = qkv[:, :q_cols]
    key_rows = qkv[:, q_cols : q_cols + k_cols]
    value_rows = qkv[:, q_cols + k_cols :]
    rim = passed_along(qkv[-window:, q_cols:], DP_AXES, 1)
    rim_keys, rim_values = rim[:, :k_cols], rim[:, k_cols:]
    first_row = (lax.axis_index("dx") * z_peers + lax.axis_index("dz")) * row_count
    ext_keys = jnp.concatenate([rim_keys, key_rows], axis=0).reshape(
        row_count + window, kv_heads, DH
    )
    ext_values = jnp.concatenate([rim_values, value_rows], axis=0).reshape(
        row_count + window, kv_heads, DH
    )
    key_blk = paired_blocks(ext_keys, window)
    value_blk = paired_blocks(ext_values, window)
    query_blk = queries.reshape(blocks, window, kv_heads, group_size, DH)
    scores = (
        jnp.einsum("bikgd,bjkd->bkgij", query_blk, key_blk, preferred_element_type=jnp.float32)
        * score_scale
    )
    allowed = band_mask(first_row, blocks, window)[:, None, None]
    scores = jnp.where(allowed, scores, masked_score)
    sink_row = sinks.reshape(kv_heads, group_size)[None, :, :, None]
    row_peak = jnp.maximum(jnp.max(scores, axis=-1), sink_row)
    row_total = jnp.exp(sink_row - row_peak) + jnp.sum(
        jnp.exp(scores - row_peak[..., None]), axis=-1
    )
    log_total = row_peak + jnp.log(row_total)
    prob_full = jnp.exp(scores - log_total[..., None])
    prob_round = prob_full.astype(jnp.bfloat16)
    attended = jnp.einsum(
        "bkgij,bjkd->bikgd", prob_round, value_blk, preferred_element_type=jnp.float32
    ).astype(jnp.bfloat16)
    attn_rows = attended.reshape(row_count, -1)
    attn_zx = by_zx(attn_rows, x_peers, z_peers)
    grad_out_part = jnp.einsum(
        "tzxi,tc->zxic", attn_zx, grad_out, preferred_element_type=jnp.float32
    ).astype(jnp.bfloat16)
    late_gathered, grad_out_part = lax.optimization_barrier((gathered, grad_out_part))
    out_over_z = lax.psum_scatter(grad_out_part, "dz", scatter_dimension=0, tiled=True)[0]
    full_out = late_gathered[:, :, in_width:].reshape((-1,) + w_out.shape[1:])
    grad_attn = contract_cols(grad_out, full_out).astype(jnp.bfloat16)
    dattn_blk = grad_attn.reshape(blocks, window, kv_heads, group_size, DH)
    row_delta = jnp.sum(
        dattn_blk.astype(jnp.float32) * attended.astype(jnp.float32), axis=-1
    ).transpose(0, 2, 3, 1)
    grad_prob = jnp.einsum(
        "bikgd,bjkd->bkgij", dattn_blk, value_blk, preferred_element_type=jnp.float32
    )
    grad_scores = (prob_full * (grad_prob - row_delta[..., None]) * score_scale).astype(
        jnp.bfloat16
    )
    grad_queries = (
        jnp.einsum("bkgij,bjkd->bikgd", grad_scores, key_blk, preferred_element_type=jnp.float32)
        .astype(jnp.bfloat16)
        .reshape(row_count, -1)
    )
    grad_key_blk = jnp.einsum(
        "bkgij,bikgd->bjkd", grad_scores, query_blk, preferred_element_type=jnp.float32
    )
    grad_value_blk = jnp.einsum(
        "bkgij,bikgd->bjkd", prob_round, dattn_blk, preferred_element_type=jnp.float32
    )
    grad_key_ext = fold_blocks(grad_key_blk, window).reshape(row_count + window, -1)
    grad_value_ext = fold_blocks(grad_value_blk, window).reshape(row_count + window, -1)
    back_rim = jnp.concatenate([grad_key_ext[:window], grad_value_ext[:window]], axis=1)
    back_rim = passed_along(back_rim.astype(jnp.bfloat16), DP_AXES, -1).astype(jnp.float32)
    back_keys, back_values = back_rim[:, :k_cols], back_rim[:, k_cols:]
    own_keys = grad_key_ext[window:]
    own_values = grad_value_ext[window:]
    grad_keys = jnp.concatenate(
        [own_keys[:-window], own_keys[-window:] + back_keys], axis=0
    ).astype(jnp.bfloat16)
    grad_values = jnp.concatenate(
        [own_values[:-window], own_values[-window:] + back_values], axis=0
    ).astype(jnp.bfloat16)
    grad_qkv = jnp.concatenate([grad_queries, grad_keys, grad_values], axis=1)
    tokens_zx = by_zx(tokens, x_peers, z_peers)
    grad_in_part = jnp.einsum(
        "tzxr,tc->zxrc", tokens_zx, grad_qkv, preferred_element_type=jnp.float32
    ).astype(jnp.bfloat16)
    token_src, grad_in_part = lax.optimization_barrier((late_gathered, grad_in_part))
    in_over_z = lax.psum_scatter(grad_in_part, "dz", scatter_dimension=0, tiled=True)[0]
    grad_wide = jnp.pad(grad_qkv, ((0, 0), (0, gathered.shape[2] - in_width)))
    proj_by_mp = token_src.reshape((mp_peers, -1) + gathered.shape[1:])
    token_terms = jnp.einsum(
        "tc,mjrc->tmjr", grad_wide, proj_by_mp, preferred_element_type=jnp.float32
    )
    grad_tokens = scatter_cols_mp(token_terms, CORES)
    out_over_z = out_over_z.reshape(x_peers, -1, in_width)
    both = jnp.concatenate([in_over_z, out_over_z], axis=1)
    over_x = scatter_rows_x(both)
    in_rows = w_query.shape[0]
    grad_in = over_x[:in_rows]
    grad_w_out = over_x[in_rows:].reshape(w_out.shape)
    grad_scale = 1.0 / math.sqrt(row_count * dp_peers)
    grad_in = grad_in * grad_scale
    return (
        grad_tokens,
        grad_in[:, :q_cols],
        grad_in[:, q_cols : q_cols + k_cols],
        grad_in[:, q_cols + k_cols :],
        grad_w_out * grad_scale,
    )


def split_mesh(mesh):
    dp = mesh.shape["dp"]
    try:
        x_peers = len({d.coords[0] for d in mesh.devices.flat})
    except AttributeError:
        x_peers = 4
    if dp % x_peers:
        x_peers = 1
    devices = mesh.devices.reshape(x_peers, dp // x_peers, mesh.shape["mp"])
    return Mesh(devices, ("dx", "dz", "mp"))


def solution(mesh):
    mesh = split_mesh(mesh)
    dp = DP_AXES
    return jax.shard_map(
        shards,
        mesh=mesh,
        in_specs=(
            P(dp, None),
            P(dp, "mp"),
            P(dp, "mp"),
            P(dp, "mp"),
            P(("mp",) + dp, None),
            P("mp"),
            P(dp, None),
        ),
        out_specs=(
            P(dp, "mp"),
            P(dp, "mp"),
            P(dp, "mp"),
            P(dp, "mp"),
            P(("mp",) + dp, None),
        ),
        check_vma=False,
    )
```

```python
import math

import jax
import jax.numpy as jnp
from jax import lax
from jax.sharding import Mesh, PartitionSpec as P

DH = 64
WINDOW = 128
LENGTH = 16384


masked_score = -1e30
DP_AXES = ("dx", "dz")
LANES = 128
CORES = 2


def passed_along(array, axis, by):
    peers = lax.axis_size(axis)
    pairs = [(i, i + by) for i in range(peers) if 0 <= i + by < peers]
    return lax.ppermute(array, axis, pairs)


def contract_rows(left_side, right_side):
    return lax.dot_general(
        left_side, right_side, (((0,), (0,)), ((), ())), preferred_element_type=jnp.float32
    )


def contract_cols(left_side, right_side):
    return lax.dot_general(
        left_side, right_side, (((1,), (1,)), ((), ())), preferred_element_type=jnp.float32
    )


def band_mask(first_row, blocks, window):
    block_ids = jnp.arange(blocks, dtype=jnp.int32)[:, None, None] * window
    query_pos = first_row + block_ids + jnp.arange(window, dtype=jnp.int32)[None, :, None]
    key_pos = (
        first_row + block_ids + jnp.arange(2 * window, dtype=jnp.int32)[None, None, :] - window
    )
    offset = query_pos - key_pos
    same_resp = jnp.floor_divide(query_pos, LENGTH) == jnp.floor_divide(key_pos, LENGTH)
    return (offset >= 0) & (offset < window) & same_resp


def paired_blocks(extended, window):
    stacked = extended.reshape((-1, window) + extended.shape[1:])
    return jnp.concatenate([stacked[:-1], stacked[1:]], axis=1)


def fold_blocks(paired, window):
    widths = [(0, 0)] * (paired.ndim - 1)
    lower_half = jnp.pad(paired[:, :window], [(0, 1)] + widths)
    upper_half = jnp.pad(paired[:, window:], [(1, 0)] + widths)
    summed = lower_half + upper_half
    return summed.reshape((summed.shape[0] * window,) + summed.shape[2:])


def rows_of(array, lead):
    return array.reshape(array.shape[:1] + lead + (-1,))


def scatter_cols_mp(terms, cores):
    peers = lax.axis_size("mp")
    chips = peers // cores
    me = lax.axis_index("mp")
    my_chip, my_core = me // cores, me % cores
    by_core = terms.reshape((terms.shape[0], chips, cores) + terms.shape[2:])
    total = lax.dynamic_index_in_dim(by_core, my_core, axis=2, keepdims=False).astype(jnp.float32)
    for shift in range(1, cores):
        dest = (my_core + shift) % cores
        piece = lax.dynamic_index_in_dim(by_core, dest, axis=2, keepdims=False)
        pairs = [(k, k - k % cores + (k % cores + shift) % cores) for k in range(peers)]
        got = lax.ppermute(piece.astype(jnp.bfloat16), "mp", pairs)
        total = total + got.astype(jnp.float32)
    result = lax.dynamic_index_in_dim(total, my_chip, axis=1, keepdims=False)
    for shift in range(1, chips):
        dest = (my_chip + shift) % chips
        piece = lax.dynamic_index_in_dim(total, dest, axis=1, keepdims=False)
        pairs = [(k, ((k // cores + shift) % chips) * cores + k % cores) for k in range(peers)]
        got = lax.ppermute(piece.astype(jnp.bfloat16), "mp", pairs)
        result = result + got.astype(jnp.float32)
    return result.reshape(result.shape[0], -1).astype(jnp.bfloat16)


def scatter_rows_x(parts):
    peers = lax.axis_size("dx")
    me = lax.axis_index("dx")
    total = lax.dynamic_index_in_dim(parts, me, axis=0, keepdims=False).astype(jnp.float32)
    for shift in range(1, peers):
        dest = (me + shift) % peers
        piece = lax.dynamic_index_in_dim(parts, dest, axis=0, keepdims=False)
        pairs = [(i, (i + shift) % peers) for i in range(peers)]
        total = total + lax.ppermute(piece, "dx", pairs).astype(jnp.float32)
    return total


def by_zx(rows, x_peers, z_peers):
    split = rows.reshape(rows.shape[0], x_peers, z_peers, -1)
    return split.transpose(0, 2, 1, 3)


def shards(tokens, w_query, w_key, w_value, w_out, sinks, grad_out):
    row_count = tokens.shape[0]
    window = WINDOW
    blocks = row_count // window
    score_scale = 1.0 / math.sqrt(DH)
    x_peers = lax.axis_size("dx")
    z_peers = lax.axis_size("dz")
    mp_peers = lax.axis_size("mp")
    dp_peers = x_peers * z_peers
    q_cols, k_cols, v_cols = w_query.shape[1], w_key.shape[1], w_value.shape[1]
    in_width = q_cols + k_cols + v_cols
    out_rows = w_out.shape[0]
    packed = jnp.concatenate(
        [w_query, w_key, w_value, w_out.reshape(w_query.shape[0], -1)], axis=1
    )
    gathered = lax.all_gather(packed, DP_AXES, axis=0, tiled=False)
    in_full = gathered[:, :, :in_width]
    kv_heads = k_cols // DH
    group_size = q_cols // DH // kv_heads
    tokens_blk = rows_of(tokens, (dp_peers,))
    qkv = jnp.einsum("tdr,drc->tc", tokens_blk, in_full, preferred_element_type=jnp.float32).astype(
        jnp.bfloat16
    )
    queries = qkv[:, :q_cols]
    key_rows = qkv[:, q_cols : q_cols + k_cols]
    value_rows = qkv[:, q_cols + k_cols :]
    rim = passed_along(qkv[-window:, q_cols:], DP_AXES, 1)
    rim_keys, rim_values = rim[:, :k_cols], rim[:, k_cols:]
    first_row = (lax.axis_index("dx") * z_peers + lax.axis_index("dz")) * row_count
    ext_keys = jnp.concatenate([rim_keys, key_rows], axis=0).reshape(
        row_count + window, kv_heads, DH
    )
    ext_values = jnp.concatenate([rim_values, value_rows], axis=0).reshape(
        row_count + window, kv_heads, DH
    )
    key_blk = paired_blocks(ext_keys, window)
    value_blk = paired_blocks(ext_values, window)
    query_blk = queries.reshape(blocks, window, kv_heads, group_size, DH)
    scores = (
        jnp.einsum("bikgd,bjkd->bkgij", query_blk, key_blk, preferred_element_type=jnp.float32)
        * score_scale
    )
    allowed = band_mask(first_row, blocks, window)[:, None, None]
    scores = jnp.where(allowed, scores, masked_score)
    sink_row = sinks.reshape(kv_heads, group_size)[None, :, :, None]
    row_peak = jnp.maximum(jnp.max(scores, axis=-1), sink_row)
    row_total = jnp.exp(sink_row - row_peak) + jnp.sum(
        jnp.exp(scores - row_peak[..., None]), axis=-1
    )
    log_total = row_peak + jnp.log(row_total)
    prob_full = jnp.exp(scores - log_total[..., None])
    prob_round = prob_full.astype(jnp.bfloat16)
    attended = jnp.einsum(
        "bkgij,bjkd->bikgd", prob_round, value_blk, preferred_element_type=jnp.float32
    ).astype(jnp.bfloat16)
    attn_rows = attended.reshape(row_count, -1)
    attn_zx = by_zx(attn_rows, x_peers, z_peers)
    grad_out_part = jnp.einsum(
        "tzxi,tc->zxic", attn_zx, grad_out, preferred_element_type=jnp.float32
    ).astype(jnp.bfloat16)
    late_gathered, grad_out_part = lax.optimization_barrier((gathered, grad_out_part))
    out_over_z = lax.psum_scatter(grad_out_part, "dz", scatter_dimension=0, tiled=True)[0]
    full_out = late_gathered[:, :, in_width:].reshape((-1,) + w_out.shape[1:])
    grad_attn = contract_cols(grad_out, full_out).astype(jnp.bfloat16)
    dattn_blk = grad_attn.reshape(blocks, window, kv_heads, group_size, DH)
    row_delta = jnp.sum(
        dattn_blk.astype(jnp.float32) * attended.astype(jnp.float32), axis=-1
    ).transpose(0, 2, 3, 1)
    grad_prob = jnp.einsum(
        "bikgd,bjkd->bkgij", dattn_blk, value_blk, preferred_element_type=jnp.float32
    )
    grad_scores = (prob_full * (grad_prob - row_delta[..., None]) * score_scale).astype(
        jnp.bfloat16
    )
    grad_queries = (
        jnp.einsum("bkgij,bjkd->bikgd", grad_scores, key_blk, preferred_element_type=jnp.float32)
        .astype(jnp.bfloat16)
        .reshape(row_count, -1)
    )
    grad_key_blk = jnp.einsum(
        "bkgij,bikgd->bjkd", grad_scores, query_blk, preferred_element_type=jnp.float32
    )
    grad_value_blk = jnp.einsum(
        "bkgij,bikgd->bjkd", prob_round, dattn_blk, preferred_element_type=jnp.float32
    )
    grad_key_ext = fold_blocks(grad_key_blk, window).reshape(row_count + window, -1)
    grad_value_ext = fold_blocks(grad_value_blk, window).reshape(row_count + window, -1)
    back_rim = jnp.concatenate([grad_key_ext[:window], grad_value_ext[:window]], axis=1)
    back_rim = passed_along(back_rim.astype(jnp.bfloat16), DP_AXES, -1).astype(jnp.float32)
    back_keys, back_values = back_rim[:, :k_cols], back_rim[:, k_cols:]
    own_keys = grad_key_ext[window:]
    own_values = grad_value_ext[window:]
    grad_keys = jnp.concatenate(
        [own_keys[:-window], own_keys[-window:] + back_keys], axis=0
    ).astype(jnp.bfloat16)
    grad_values = jnp.concatenate(
        [own_values[:-window], own_values[-window:] + back_values], axis=0
    ).astype(jnp.bfloat16)
    grad_qkv = jnp.concatenate([grad_queries, grad_keys, grad_values], axis=1)
    tokens_zx = by_zx(tokens, x_peers, z_peers)
    grad_in_part = jnp.einsum(
        "tzxr,tc->zxrc", tokens_zx, grad_qkv, preferred_element_type=jnp.float32
    ).astype(jnp.bfloat16)
    token_src, out_over_z, grad_in_part = lax.optimization_barrier(
        (late_gathered, out_over_z, grad_in_part)
    )
    in_over_z = lax.psum_scatter(grad_in_part, "dz", scatter_dimension=0, tiled=True)[0]
    grad_wide = jnp.pad(grad_qkv, ((0, 0), (0, gathered.shape[2] - in_width)))
    proj_by_mp = token_src.reshape((mp_peers, -1) + gathered.shape[1:])
    token_terms = jnp.einsum(
        "tc,mjrc->tmjr", grad_wide, proj_by_mp, preferred_element_type=jnp.float32
    )
    grad_tokens = scatter_cols_mp(token_terms, CORES)
    grad_w_out = scatter_rows_x(out_over_z)
    grad_in = scatter_rows_x(in_over_z)
    grad_scale = 1.0 / math.sqrt(row_count * dp_peers)
    grad_in = grad_in * grad_scale
    return (
        grad_tokens,
        grad_in[:, :q_cols],
        grad_in[:, q_cols : q_cols + k_cols],
        grad_in[:, q_cols + k_cols :],
        grad_w_out * grad_scale,
    )


def split_mesh(mesh):
    dp = mesh.shape["dp"]
    try:
        x_peers = len({d.coords[0] for d in mesh.devices.flat})
    except AttributeError:
        x_peers = 4
    if dp % x_peers:
        x_peers = 1
    devices = mesh.devices.reshape(x_peers, dp // x_peers, mesh.shape["mp"])
    return Mesh(devices, ("dx", "dz", "mp"))


def solution(mesh):
    mesh = split_mesh(mesh)
    dp = DP_AXES
    return jax.shard_map(
        shards,
        mesh=mesh,
        in_specs=(
            P(dp, None),
            P(dp, "mp"),
            P(dp, "mp"),
            P(dp, "mp"),
            P(("mp",) + dp, None),
            P("mp"),
            P(dp, None),
        ),
        out_specs=(
            P(dp, "mp"),
            P(dp, "mp"),
            P(dp, "mp"),
            P(dp, "mp"),
            P(("mp",) + dp, None),
        ),
        check_vma=False,
    )
```

```python
import math

import jax
import jax.numpy as jnp
from jax import lax
from jax.sharding import Mesh, PartitionSpec as P

DH = 64
WINDOW = 128
LENGTH = 16384


masked_score = -1e30
DP_AXES = ("dx", "dz")
LANES = 128
CORES = 2


def passed_along(array, axis, by):
    peers = lax.axis_size(axis)
    pairs = [(i, i + by) for i in range(peers) if 0 <= i + by < peers]
    return lax.ppermute(array, axis, pairs)


def contract_rows(left_side, right_side):
    return lax.dot_general(
        left_side, right_side, (((0,), (0,)), ((), ())), preferred_element_type=jnp.float32
    )


def contract_cols(left_side, right_side):
    return lax.dot_general(
        left_side, right_side, (((1,), (1,)), ((), ())), preferred_element_type=jnp.float32
    )


def band_mask(first_row, blocks, window):
    block_ids = jnp.arange(blocks, dtype=jnp.int32)[:, None, None] * window
    query_pos = first_row + block_ids + jnp.arange(window, dtype=jnp.int32)[None, :, None]
    key_pos = (
        first_row + block_ids + jnp.arange(2 * window, dtype=jnp.int32)[None, None, :] - window
    )
    offset = query_pos - key_pos
    same_resp = jnp.floor_divide(query_pos, LENGTH) == jnp.floor_divide(key_pos, LENGTH)
    return (offset >= 0) & (offset < window) & same_resp


def paired_blocks(extended, window):
    stacked = extended.reshape((-1, window) + extended.shape[1:])
    return jnp.concatenate([stacked[:-1], stacked[1:]], axis=1)


def fold_blocks(paired, window):
    widths = [(0, 0)] * (paired.ndim - 1)
    lower_half = jnp.pad(paired[:, :window], [(0, 1)] + widths)
    upper_half = jnp.pad(paired[:, window:], [(1, 0)] + widths)
    summed = lower_half + upper_half
    return summed.reshape((summed.shape[0] * window,) + summed.shape[2:])


def rows_of(array, lead):
    return array.reshape(array.shape[:1] + lead + (-1,))


def scatter_cols_mp(terms, cores):
    peers = lax.axis_size("mp")
    chips = peers // cores
    me = lax.axis_index("mp")
    my_chip, my_core = me // cores, me % cores
    by_core = terms.reshape((terms.shape[0], chips, cores) + terms.shape[2:])
    total = lax.dynamic_index_in_dim(by_core, my_core, axis=2, keepdims=False).astype(jnp.float32)
    for shift in range(1, cores):
        dest = (my_core + shift) % cores
        piece = lax.dynamic_index_in_dim(by_core, dest, axis=2, keepdims=False)
        pairs = [(k, k - k % cores + (k % cores + shift) % cores) for k in range(peers)]
        got = lax.ppermute(piece.astype(jnp.bfloat16), "mp", pairs)
        total = total + got.astype(jnp.float32)
    result = lax.dynamic_index_in_dim(total, my_chip, axis=1, keepdims=False)
    for shift in range(1, chips):
        dest = (my_chip + shift) % chips
        piece = lax.dynamic_index_in_dim(total, dest, axis=1, keepdims=False)
        pairs = [(k, ((k // cores + shift) % chips) * cores + k % cores) for k in range(peers)]
        got = lax.ppermute(piece.astype(jnp.bfloat16), "mp", pairs)
        result = result + got.astype(jnp.float32)
    return result.reshape(result.shape[0], -1).astype(jnp.bfloat16)


def scatter_rows_x(parts):
    peers = lax.axis_size("dx")
    me = lax.axis_index("dx")
    total = lax.dynamic_index_in_dim(parts, me, axis=0, keepdims=False).astype(jnp.float32)
    for shift in range(1, peers):
        dest = (me + shift) % peers
        piece = lax.dynamic_index_in_dim(parts, dest, axis=0, keepdims=False)
        pairs = [(i, (i + shift) % peers) for i in range(peers)]
        total = total + lax.ppermute(piece, "dx", pairs).astype(jnp.float32)
    return total


def by_zx(rows, x_peers, z_peers):
    split = rows.reshape(rows.shape[0], x_peers, z_peers, -1)
    return split.transpose(0, 2, 1, 3)


def shards(tokens, w_query, w_key, w_value, w_out, sinks, grad_out):
    row_count = tokens.shape[0]
    window = WINDOW
    blocks = row_count // window
    score_scale = 1.0 / math.sqrt(DH)
    x_peers = lax.axis_size("dx")
    z_peers = lax.axis_size("dz")
    mp_peers = lax.axis_size("mp")
    dp_peers = x_peers * z_peers
    q_cols, k_cols, v_cols = w_query.shape[1], w_key.shape[1], w_value.shape[1]
    in_width = q_cols + k_cols + v_cols
    out_rows = w_out.shape[0]
    packed = jnp.concatenate(
        [w_query, w_key, w_value, w_out.reshape(w_query.shape[0], -1)], axis=1
    )
    gathered = lax.all_gather(packed, DP_AXES, axis=0, tiled=False)
    in_full = gathered[:, :, :in_width]
    kv_heads = k_cols // DH
    group_size = q_cols // DH // kv_heads
    tokens_blk = rows_of(tokens, (dp_peers,))
    qkv = jnp.einsum("tdr,drc->tc", tokens_blk, in_full, preferred_element_type=jnp.float32).astype(
        jnp.bfloat16
    )
    queries = qkv[:, :q_cols]
    key_rows = qkv[:, q_cols : q_cols + k_cols]
    value_rows = qkv[:, q_cols + k_cols :]
    rim = passed_along(qkv[-window:, q_cols:], DP_AXES, 1)
    rim_keys, rim_values = rim[:, :k_cols], rim[:, k_cols:]
    first_row = (lax.axis_index("dx") * z_peers + lax.axis_index("dz")) * row_count
    ext_keys = jnp.concatenate([rim_keys, key_rows], axis=0).reshape(
        row_count + window, kv_heads, DH
    )
    ext_values = jnp.concatenate([rim_values, value_rows], axis=0).reshape(
        row_count + window, kv_heads, DH
    )
    key_blk = paired_blocks(ext_keys, window)
    value_blk = paired_blocks(ext_values, window)
    query_blk = queries.reshape(blocks, window, kv_heads, group_size, DH)
    scores = (
        jnp.einsum("bikgd,bjkd->bkgij", query_blk, key_blk, preferred_element_type=jnp.float32)
        * score_scale
    )
    allowed = band_mask(first_row, blocks, window)[:, None, None]
    scores = jnp.where(allowed, scores, masked_score)
    sink_row = sinks.reshape(kv_heads, group_size)[None, :, :, None]
    row_peak = jnp.maximum(jnp.max(scores, axis=-1), sink_row)
    row_total = jnp.exp(sink_row - row_peak) + jnp.sum(
        jnp.exp(scores - row_peak[..., None]), axis=-1
    )
    log_total = row_peak + jnp.log(row_total)
    prob_full = jnp.exp(scores - log_total[..., None])
    prob_round = prob_full.astype(jnp.bfloat16)
    attended = jnp.einsum(
        "bkgij,bjkd->bikgd", prob_round, value_blk, preferred_element_type=jnp.float32
    ).astype(jnp.bfloat16)
    attn_rows = attended.reshape(row_count, -1)
    attn_zx = by_zx(attn_rows, x_peers, z_peers)
    grad_out_part = jnp.einsum(
        "tzxi,tc->zxic", attn_zx, grad_out, preferred_element_type=jnp.float32
    ).astype(jnp.bfloat16)
    late_gathered, grad_out_part = lax.optimization_barrier((gathered, grad_out_part))
    out_over_z = lax.psum_scatter(grad_out_part, "dz", scatter_dimension=0, tiled=True)[0]
    full_out = late_gathered[:, :, in_width:].reshape((-1,) + w_out.shape[1:])
    grad_attn = contract_cols(grad_out, full_out).astype(jnp.bfloat16)
    dattn_blk = grad_attn.reshape(blocks, window, kv_heads, group_size, DH)
    row_delta = jnp.sum(
        dattn_blk.astype(jnp.float32) * attended.astype(jnp.float32), axis=-1
    ).transpose(0, 2, 3, 1)
    grad_prob = jnp.einsum(
        "bikgd,bjkd->bkgij", dattn_blk, value_blk, preferred_element_type=jnp.float32
    )
    grad_scores = (prob_full * (grad_prob - row_delta[..., None]) * score_scale).astype(
        jnp.bfloat16
    )
    grad_queries = (
        jnp.einsum("bkgij,bjkd->bikgd", grad_scores, key_blk, preferred_element_type=jnp.float32)
        .astype(jnp.bfloat16)
        .reshape(row_count, -1)
    )
    grad_key_blk = jnp.einsum(
        "bkgij,bikgd->bjkd", grad_scores, query_blk, preferred_element_type=jnp.float32
    )
    grad_value_blk = jnp.einsum(
        "bkgij,bikgd->bjkd", prob_round, dattn_blk, preferred_element_type=jnp.float32
    )
    grad_key_ext = fold_blocks(grad_key_blk, window).reshape(row_count + window, -1)
    grad_value_ext = fold_blocks(grad_value_blk, window).reshape(row_count + window, -1)
    back_rim = jnp.concatenate([grad_key_ext[:window], grad_value_ext[:window]], axis=1)
    back_rim = passed_along(back_rim.astype(jnp.bfloat16), DP_AXES, -1).astype(jnp.float32)
    back_keys, back_values = back_rim[:, :k_cols], back_rim[:, k_cols:]
    own_keys = grad_key_ext[window:]
    own_values = grad_value_ext[window:]
    grad_keys = jnp.concatenate(
        [own_keys[:-window], own_keys[-window:] + back_keys], axis=0
    ).astype(jnp.bfloat16)
    grad_values = jnp.concatenate(
        [own_values[:-window], own_values[-window:] + back_values], axis=0
    ).astype(jnp.bfloat16)
    grad_qkv = jnp.concatenate([grad_queries, grad_keys, grad_values], axis=1)
    tokens_zx = by_zx(tokens, x_peers, z_peers)
    grad_in_part = jnp.einsum(
        "tzxr,tc->zxrc", tokens_zx, grad_qkv, preferred_element_type=jnp.float32
    ).astype(jnp.bfloat16)
    token_src, out_over_z, grad_in_part = lax.optimization_barrier(
        (late_gathered, out_over_z, grad_in_part)
    )
    in_over_z = lax.psum_scatter(grad_in_part, "dz", scatter_dimension=0, tiled=True)[0]
    grad_wide = jnp.pad(grad_qkv, ((0, 0), (0, gathered.shape[2] - in_width)))
    proj_by_mp = token_src.reshape((mp_peers, -1) + gathered.shape[1:])
    token_terms = jnp.einsum(
        "tc,mjrc->tmjr", grad_wide, proj_by_mp, preferred_element_type=jnp.float32
    )
    grad_tokens = scatter_cols_mp(token_terms, CORES)
    grad_w_out = scatter_rows_x(out_over_z)
    grad_in = jnp.sum(
        lax.all_to_all(in_over_z, "dx", 0, 0, tiled=True).astype(jnp.float32), axis=0
    )
    grad_scale = 1.0 / math.sqrt(row_count * dp_peers)
    grad_in = grad_in * grad_scale
    return (
        grad_tokens,
        grad_in[:, :q_cols],
        grad_in[:, q_cols : q_cols + k_cols],
        grad_in[:, q_cols + k_cols :],
        grad_w_out * grad_scale,
    )


def split_mesh(mesh):
    dp = mesh.shape["dp"]
    try:
        x_peers = len({d.coords[0] for d in mesh.devices.flat})
    except AttributeError:
        x_peers = 4
    if dp % x_peers:
        x_peers = 1
    devices = mesh.devices.reshape(x_peers, dp // x_peers, mesh.shape["mp"])
    return Mesh(devices, ("dx", "dz", "mp"))


def solution(mesh):
    mesh = split_mesh(mesh)
    dp = DP_AXES
    return jax.shard_map(
        shards,
        mesh=mesh,
        in_specs=(
            P(dp, None),
            P(dp, "mp"),
            P(dp, "mp"),
            P(dp, "mp"),
            P(("mp",) + dp, None),
            P("mp"),
            P(dp, None),
        ),
        out_specs=(
            P(dp, "mp"),
            P(dp, "mp"),
            P(dp, "mp"),
            P(dp, "mp"),
            P(("mp",) + dp, None),
        ),
        check_vma=False,
    )
```

```python
import math

import jax
import jax.numpy as jnp
from jax import lax
from jax.sharding import Mesh, PartitionSpec as P

DH = 64
WINDOW = 128
LENGTH = 16384


masked_score = -1e30
DP_AXES = ("dx", "dz")
LANES = 128
CORES = 2


def passed_along(array, axis, by):
    peers = lax.axis_size(axis)
    pairs = [(i, i + by) for i in range(peers) if 0 <= i + by < peers]
    return lax.ppermute(array, axis, pairs)


def contract_rows(left_side, right_side):
    return lax.dot_general(
        left_side, right_side, (((0,), (0,)), ((), ())), preferred_element_type=jnp.float32
    )


def contract_cols(left_side, right_side):
    return lax.dot_general(
        left_side, right_side, (((1,), (1,)), ((), ())), preferred_element_type=jnp.float32
    )


def band_mask(first_row, blocks, window):
    block_ids = jnp.arange(blocks, dtype=jnp.int32)[:, None, None] * window
    query_pos = first_row + block_ids + jnp.arange(window, dtype=jnp.int32)[None, :, None]
    key_pos = (
        first_row + block_ids + jnp.arange(2 * window, dtype=jnp.int32)[None, None, :] - window
    )
    offset = query_pos - key_pos
    same_resp = jnp.floor_divide(query_pos, LENGTH) == jnp.floor_divide(key_pos, LENGTH)
    return (offset >= 0) & (offset < window) & same_resp


def paired_blocks(extended, window):
    stacked = extended.reshape((-1, window) + extended.shape[1:])
    return jnp.concatenate([stacked[:-1], stacked[1:]], axis=1)


def fold_blocks(paired, window):
    widths = [(0, 0)] * (paired.ndim - 1)
    lower_half = jnp.pad(paired[:, :window], [(0, 1)] + widths)
    upper_half = jnp.pad(paired[:, window:], [(1, 0)] + widths)
    summed = lower_half + upper_half
    return summed.reshape((summed.shape[0] * window,) + summed.shape[2:])


def rows_of(array, lead):
    return array.reshape(array.shape[:1] + lead + (-1,))


def scatter_cols_mp(terms, cores):
    peers = lax.axis_size("mp")
    chips = peers // cores
    me = lax.axis_index("mp")
    my_chip, my_core = me // cores, me % cores
    by_core = terms.reshape((terms.shape[0], chips, cores) + terms.shape[2:])
    total = lax.dynamic_index_in_dim(by_core, my_core, axis=2, keepdims=False).astype(jnp.float32)
    for shift in range(1, cores):
        dest = (my_core + shift) % cores
        piece = lax.dynamic_index_in_dim(by_core, dest, axis=2, keepdims=False)
        pairs = [(k, k - k % cores + (k % cores + shift) % cores) for k in range(peers)]
        got = lax.ppermute(piece.astype(jnp.bfloat16), "mp", pairs)
        total = total + got.astype(jnp.float32)
    result = lax.dynamic_index_in_dim(total, my_chip, axis=1, keepdims=False)
    for shift in range(1, chips):
        dest = (my_chip + shift) % chips
        piece = lax.dynamic_index_in_dim(total, dest, axis=1, keepdims=False)
        pairs = [(k, ((k // cores + shift) % chips) * cores + k % cores) for k in range(peers)]
        got = lax.ppermute(piece.astype(jnp.bfloat16), "mp", pairs)
        result = result + got.astype(jnp.float32)
    return result.reshape(result.shape[0], -1).astype(jnp.bfloat16)


def scatter_rows_x(parts):
    peers = lax.axis_size("dx")
    me = lax.axis_index("dx")
    total = lax.dynamic_index_in_dim(parts, me, axis=0, keepdims=False).astype(jnp.float32)
    for shift in range(1, peers):
        dest = (me + shift) % peers
        piece = lax.dynamic_index_in_dim(parts, dest, axis=0, keepdims=False)
        pairs = [(i, (i + shift) % peers) for i in range(peers)]
        total = total + lax.ppermute(piece, "dx", pairs).astype(jnp.float32)
    return total


def by_zx(rows, x_peers, z_peers):
    split = rows.reshape(rows.shape[0], x_peers, z_peers, -1)
    return split.transpose(0, 2, 1, 3)


def shards(tokens, w_query, w_key, w_value, w_out, sinks, grad_out):
    row_count = tokens.shape[0]
    window = WINDOW
    blocks = row_count // window
    score_scale = 1.0 / math.sqrt(DH)
    x_peers = lax.axis_size("dx")
    z_peers = lax.axis_size("dz")
    mp_peers = lax.axis_size("mp")
    dp_peers = x_peers * z_peers
    q_cols, k_cols, v_cols = w_query.shape[1], w_key.shape[1], w_value.shape[1]
    in_width = q_cols + k_cols + v_cols
    out_rows = w_out.shape[0]
    packed = jnp.concatenate(
        [w_query, w_key, w_value, w_out.reshape(w_query.shape[0], -1)], axis=1
    )
    gathered = lax.all_gather(packed, DP_AXES, axis=0, tiled=False)
    in_full = gathered[:, :, :in_width]
    kv_heads = k_cols // DH
    group_size = q_cols // DH // kv_heads
    tokens_blk = rows_of(tokens, (dp_peers,))
    qkv = jnp.einsum("tdr,drc->tc", tokens_blk, in_full, preferred_element_type=jnp.float32).astype(
        jnp.bfloat16
    )
    queries = qkv[:, :q_cols]
    key_rows = qkv[:, q_cols : q_cols + k_cols]
    value_rows = qkv[:, q_cols + k_cols :]
    rim = passed_along(qkv[-window:, q_cols:], DP_AXES, 1)
    rim_keys, rim_values = rim[:, :k_cols], rim[:, k_cols:]
    first_row = (lax.axis_index("dx") * z_peers + lax.axis_index("dz")) * row_count
    ext_keys = jnp.concatenate([rim_keys, key_rows], axis=0).reshape(
        row_count + window, kv_heads, DH
    )
    ext_values = jnp.concatenate([rim_values, value_rows], axis=0).reshape(
        row_count + window, kv_heads, DH
    )
    key_blk = paired_blocks(ext_keys, window)
    value_blk = paired_blocks(ext_values, window)
    query_blk = queries.reshape(blocks, window, kv_heads, group_size, DH)
    scores = (
        jnp.einsum("bikgd,bjkd->bkgij", query_blk, key_blk, preferred_element_type=jnp.float32)
        * score_scale
    )
    allowed = band_mask(first_row, blocks, window)[:, None, None]
    scores = jnp.where(allowed, scores, masked_score)
    sink_row = sinks.reshape(kv_heads, group_size)[None, :, :, None]
    row_peak = jnp.maximum(jnp.max(scores, axis=-1), sink_row)
    row_total = jnp.exp(sink_row - row_peak) + jnp.sum(
        jnp.exp(scores - row_peak[..., None]), axis=-1
    )
    log_total = row_peak + jnp.log(row_total)
    prob_full = jnp.exp(scores - log_total[..., None])
    prob_round = prob_full.astype(jnp.bfloat16)
    attended = jnp.einsum(
        "bkgij,bjkd->bikgd", prob_round, value_blk, preferred_element_type=jnp.float32
    ).astype(jnp.bfloat16)
    attn_rows = attended.reshape(row_count, -1)
    attn_zx = by_zx(attn_rows, x_peers, z_peers)
    grad_out_part = jnp.einsum(
        "tzxi,tc->zxic", attn_zx, grad_out, preferred_element_type=jnp.float32
    ).astype(jnp.bfloat16)
    late_gathered, grad_out_part = lax.optimization_barrier((gathered, grad_out_part))
    out_over_z = lax.psum_scatter(grad_out_part, "dz", scatter_dimension=0, tiled=True)[0]
    full_out = late_gathered[:, :, in_width:].reshape((-1,) + w_out.shape[1:])
    grad_attn = contract_cols(grad_out, full_out).astype(jnp.bfloat16)
    dattn_blk = grad_attn.reshape(blocks, window, kv_heads, group_size, DH)
    row_delta = jnp.sum(
        dattn_blk.astype(jnp.float32) * attended.astype(jnp.float32), axis=-1
    ).transpose(0, 2, 3, 1)
    grad_prob = jnp.einsum(
        "bikgd,bjkd->bkgij", dattn_blk, value_blk, preferred_element_type=jnp.float32
    )
    grad_scores = (prob_full * (grad_prob - row_delta[..., None]) * score_scale).astype(
        jnp.bfloat16
    )
    grad_queries = (
        jnp.einsum("bkgij,bjkd->bikgd", grad_scores, key_blk, preferred_element_type=jnp.float32)
        .astype(jnp.bfloat16)
        .reshape(row_count, -1)
    )
    grad_key_blk = jnp.einsum(
        "bkgij,bikgd->bjkd", grad_scores, query_blk, preferred_element_type=jnp.float32
    )
    grad_value_blk = jnp.einsum(
        "bkgij,bikgd->bjkd", prob_round, dattn_blk, preferred_element_type=jnp.float32
    )
    grad_key_ext = fold_blocks(grad_key_blk, window).reshape(row_count + window, -1)
    grad_value_ext = fold_blocks(grad_value_blk, window).reshape(row_count + window, -1)
    back_rim = jnp.concatenate([grad_key_ext[:window], grad_value_ext[:window]], axis=1)
    back_rim = passed_along(back_rim.astype(jnp.bfloat16), DP_AXES, -1).astype(jnp.float32)
    back_keys, back_values = back_rim[:, :k_cols], back_rim[:, k_cols:]
    own_keys = grad_key_ext[window:]
    own_values = grad_value_ext[window:]
    grad_keys = jnp.concatenate(
        [own_keys[:-window], own_keys[-window:] + back_keys], axis=0
    ).astype(jnp.bfloat16)
    grad_values = jnp.concatenate(
        [own_values[:-window], own_values[-window:] + back_values], axis=0
    ).astype(jnp.bfloat16)
    grad_qkv = jnp.concatenate([grad_queries, grad_keys, grad_values], axis=1)
    tokens_zx = by_zx(tokens, x_peers, z_peers)
    grad_in_part = jnp.einsum(
        "tzxr,tc->zxrc", tokens_zx, grad_qkv, preferred_element_type=jnp.float32
    ).astype(jnp.bfloat16)
    token_src, out_over_z, grad_in_part = lax.optimization_barrier(
        (late_gathered, out_over_z, grad_in_part)
    )
    in_over_z = lax.psum_scatter(grad_in_part, "dz", scatter_dimension=0, tiled=True)[0]
    grad_wide = jnp.pad(grad_qkv, ((0, 0), (0, gathered.shape[2] - in_width)))
    proj_by_mp = token_src.reshape((mp_peers, -1) + gathered.shape[1:])
    token_terms = jnp.einsum(
        "tc,mjrc->tmjr", grad_wide, proj_by_mp, preferred_element_type=jnp.float32
    )
    grad_tokens = scatter_cols_mp(token_terms, CORES)
    grad_w_out = jnp.sum(
        lax.all_to_all(out_over_z, "dx", 0, 0, tiled=True).astype(jnp.float32), axis=0
    )
    grad_in = jnp.sum(
        lax.all_to_all(in_over_z, "dx", 0, 0, tiled=True).astype(jnp.float32), axis=0
    )
    grad_scale = 1.0 / math.sqrt(row_count * dp_peers)
    grad_in = grad_in * grad_scale
    return (
        grad_tokens,
        grad_in[:, :q_cols],
        grad_in[:, q_cols : q_cols + k_cols],
        grad_in[:, q_cols + k_cols :],
        grad_w_out * grad_scale,
    )


def split_mesh(mesh):
    dp = mesh.shape["dp"]
    try:
        x_peers = len({d.coords[0] for d in mesh.devices.flat})
    except AttributeError:
        x_peers = 4
    if dp % x_peers:
        x_peers = 1
    devices = mesh.devices.reshape(x_peers, dp // x_peers, mesh.shape["mp"])
    return Mesh(devices, ("dx", "dz", "mp"))


def solution(mesh):
    mesh = split_mesh(mesh)
    dp = DP_AXES
    return jax.shard_map(
        shards,
        mesh=mesh,
        in_specs=(
            P(dp, None),
            P(dp, "mp"),
            P(dp, "mp"),
            P(dp, "mp"),
            P(("mp",) + dp, None),
            P("mp"),
            P(dp, None),
        ),
        out_specs=(
            P(dp, "mp"),
            P(dp, "mp"),
            P(dp, "mp"),
            P(dp, "mp"),
            P(("mp",) + dp, None),
        ),
        check_vma=False,
    )
```
